256 devices in a mesh: gx: 8 (over x, core), gy: 4 (over y), gz: 8 (over z).
Axes of the slice: x: 4, y: 4, z: 8, core: 2. Of those that a mesh axis runs over, the one named last changes fastest.
Arguments:
- e_field: float32 [3, 256, 64, 1024], P(None, 'gx', 'gy', 'gz'), may hold values from -6 to 6
- h_field: float32 [3, 256, 64, 1024], P(None, 'gx', 'gy', 'gz'), may hold values from -6 to 6
- inv_permittivity: float32 [256, 64, 1024], P('gx', 'gy', 'gz'), may hold values from 0.0833 to 1
- dft_sums: float32 [32, 256, 64, 128], P('gz', 'gx', 'gy'), may hold values from -6 to 6
- omega: float32 [16], replicated, may hold values from 0.2 to 3
- port_z: int32 [32], P('gz'), may hold values from 0 to 1023, as said below
- mode_profiles: bfloat16 [32, 2, 4, 256, 64], P('gz'), may hold values from -0.0234375 to 0.0234375
Outputs:
- e_out: float32 [3, 256, 64, 1024], P(None, 'gx', 'gy', 'gz')
- h_out: float32 [3, 256, 64, 1024], P(None, 'gx', 'gy', 'gz')
- dft_out: float32 [32, 256, 64, 128], P('gz', 'gx', 'gy')
- intersections: float32 [64, 8, 4], P(('gx', 'gy'), 'gz')
The draws below stay inside these ranges and needn't reach their ends.
Inputs may be any that keep to these rules, and one draw needn't show every extreme that they name: `port_z`: port k lies in the slab of the third dimension that holds cells k // 4 * 128 to that plus 128 - 1.
All inputs are finite; a program needn't handle non-finite values.
Results may differ from the reference program's by a relative error of at most 0.0003.
Values sent between devices are 32-bit elements; how exact they have to be, the bound alone decides.
No kernel may reach another device: no remote copies, remote signals or barrier semaphores. Data moves between devices by JAX's collectives and lax.ppermute only.
A program may use at most 64 MiB of HBM per device.

```python
import math
import jax
import jax.numpy as jnp
from jax import lax

CZ = 128
STEPS = 2
PORTS_DEV = 4
NF = 16
MODES = 2
WAVE = 128
NX = 256
NY = 64
NZ = 1024
PORTS = 32
N_GZ = 8


def draw_port_z(key, part):
    offsets = jax.random.randint(key, (PORTS,), 0, CZ)
    offsets = offsets.at[0].set(0).at[PORTS - 1].set(CZ - 1)
    return (jnp.arange(PORTS) // PORTS_DEV * CZ + offsets).astype(jnp.int32)


def levels(key, extent, pieces, low, high):
    level, own = 1.0, jax.random.fold_in(key, 6)
    for dim, parts in pieces:
        heights = jnp.exp(jax.random.uniform(jax.random.fold_in(own, dim), (parts,), jnp.float32, low / len(pieces), high / len(pieces)))
        level = level * jnp.repeat(heights, extent[dim] // parts).reshape([-1 if axis == dim else 1 for axis in range(len(extent))])
    return level


def noise(stream_key, shape, deviation, limit, split=(), dtype=jnp.bfloat16):
    loudness = levels(stream_key, shape, split, -0.22, 0.18) if split else 1.0
    drawn = jax.random.normal(stream_key, shape, jnp.float32) * deviation * loudness
    return jnp.minimum(jnp.maximum(drawn, -limit), limit).astype(dtype)


def setup_inputs(seed: int = 0) -> dict:
    key_list = jax.random.split(jax.random.key(seed), 8)
    e_field = noise(key_list[0], (3, NX, NY, NZ), 1.0, 6.0, ((1, 8), (2, 4), (3, 8)), jnp.float32)
    h_field = noise(key_list[1], (3, NX, NY, NZ), 1.0, 6.0, ((1, 8), (2, 4), (3, 8)), jnp.float32)
    inv_permittivity = jnp.clip(jnp.exp(math.log(1.0) - 2.4853067 * jax.random.uniform(key_list[2], (NX, NY, NZ), jnp.float32) ** levels(key_list[2], (NX, NY, NZ), ((0, 8), (1, 4), (2, 8)), -0.2, 0.2)), 0.0833, 1.0)
    dft_sums = noise(key_list[3], (PORTS, NX, NY, WAVE), 1.0, 6.0, ((0, 8), (1, 8), (2, 4)), jnp.float32)
    omega = jnp.clip(jax.random.uniform(key_list[4], (NF,), jnp.float32, 0.2, 3.0), 0.2, 3.0)
    port_z = draw_port_z(jax.random.fold_in(key_list[7], 71), 0)
    mode_profiles = noise(key_list[6], (PORTS, MODES, 4, NX, NY), (4 * NX * NY) ** -0.5, 0.0234375, ((0, 8),))
    return {"e_field": e_field, "h_field": h_field, "inv_permittivity": inv_permittivity, "dft_sums": dft_sums, "omega": omega, "port_z": port_z, "mode_profiles": mode_profiles}


def forward(part, dim):
    rest = lax.slice_in_dim(part, 1, part.shape[dim], axis=dim)
    after = jnp.zeros_like(lax.slice_in_dim(part, 0, 1, axis=dim))
    return jnp.concatenate([rest, after], axis=dim) - part


def backward(part, dim):
    rest = lax.slice_in_dim(part, 0, part.shape[dim] - 1, axis=dim)
    before = jnp.zeros_like(lax.slice_in_dim(part, 0, 1, axis=dim))
    return part - jnp.concatenate([before, rest], axis=dim)


def curl(field, differ):
    along_x = differ(field[1:3], 1)
    along_y = differ(jnp.stack([field[0], field[2]]), 2)
    along_z = differ(field[0:2], 3)
    return jnp.stack([along_y[1] - along_z[1], along_z[0] - along_x[1], along_x[0] - along_y[0]])


def reference(e_field, h_field, inv_permittivity, dft_sums, omega, port_z, mode_profiles):
    e_now = e_field
    h_now = h_field
    dft = dft_sums
    for step in range(STEPS):
        h_now = h_now - 0.5 * curl(e_now, forward)
        e_now = e_now + 0.5 * inv_permittivity * curl(h_now, backward)
        tangent = jnp.stack([e_now[0], e_now[1], h_now[0], h_now[1]])
        planes = jnp.transpose(jnp.take(tangent, port_z, axis=3), (3, 1, 2, 0))
        phase = omega * jnp.float32(step + 1)
        trig = jnp.stack([jnp.cos(phase), jnp.sin(phase)])
        increment = planes[:, :, :, :, None, None] * trig[None, None, None, None, :, :]
        dft = dft + increment.reshape(dft.shape)
    shaped = dft.reshape(PORTS, NX, NY, 4, 2, NF)
    ov = jnp.einsum('kxycqf,kmcxy->kfmq', shaped, mode_profiles.astype(jnp.float32), precision=lax.Precision.HIGHEST)
    ov = ov.reshape(N_GZ, PORTS_DEV, NF, MODES * 2)
    intersections = jnp.transpose(ov, (1, 2, 0, 3)).reshape(PORTS_DEV * NF, N_GZ, MODES * 2)
    return e_now, h_now, dft, intersections
```

```python
import jax
import jax.numpy as jnp
from jax import lax
from jax.sharding import PartitionSpec as P

STEPS = 2
NF = 16
MODES = 2


def shifted(value, axis, steps):
    count = lax.axis_size(axis)
    first, last = (max(0, -steps), min(count, count - steps))
    return lax.ppermute(value, axis, [(source, source + steps) for source in range(first, last)])


def rim_x(face, offset):
    return shifted(face, "gx", offset)


def rim_y(face, offset):
    return shifted(face, "gy", offset)


def rim_z(face, offset):
    return shifted(face, "gz", offset)


def forward(part, dim, mover):
    first = lax.slice_in_dim(part, 0, 1, axis=dim)
    after = mover(first, -1)
    rest = lax.slice_in_dim(part, 1, part.shape[dim], axis=dim)
    return jnp.concatenate([rest, after], axis=dim) - part


def backward(part, dim, mover):
    count = part.shape[dim]
    last = lax.slice_in_dim(part, count - 1, count, axis=dim)
    before = mover(last, 1)
    rest = lax.slice_in_dim(part, 0, count - 1, axis=dim)
    return part - jnp.concatenate([before, rest], axis=dim)


def curl(field, differ):
    along_x = differ(field[1:3], 1, rim_x)
    along_y = differ(jnp.stack([field[0], field[2]]), 2, rim_y)
    along_z = differ(field[0:2], 3, rim_z)
    return jnp.stack([along_y[1] - along_z[1], along_z[0] - along_x[1], along_x[0] - along_y[0]])


def per_device(e_field, h_field, inv_permittivity, dft_sums, omega, port_z, mode_profiles):
    cells_x = e_field.shape[1]
    cells_y = e_field.shape[2]
    cells_z = e_field.shape[3]
    ports_here = dft_sums.shape[0]
    local_z = port_z - lax.axis_index("gz") * cells_z
    select = (local_z[:, None] == jnp.arange(cells_z)[None, :]).astype(jnp.float32)
    e_now = e_field
    h_now = h_field
    dft = dft_sums
    for step in range(STEPS):
        h_now = h_now - 0.5 * curl(e_now, forward)
        e_now = e_now + 0.5 * inv_permittivity * curl(h_now, backward)
        tangent = jnp.stack([e_now[0], e_now[1], h_now[0], h_now[1]])
        planes = jnp.einsum("cxyz,pz->pxyc", tangent, select, precision=lax.Precision.HIGHEST)
        phase = omega * jnp.float32(step + 1)
        trig = jnp.stack([jnp.cos(phase), jnp.sin(phase)])
        increment = planes[:, :, :, :, None, None] * trig[None, None, None, None, :, :]
        dft = dft + increment.reshape(dft.shape)
    shaped = dft.reshape(ports_here, cells_x, cells_y, 4, 2, NF)
    groups = lax.axis_size(("gx", "gy"))
    owned = ports_here * NF // groups
    start_x = lax.axis_index("gx") * cells_x
    start_y = lax.axis_index("gy") * cells_y
    tile = lax.dynamic_slice(
        mode_profiles, (0, 0, 0, start_x, start_y), (ports_here, MODES, 4, cells_x, cells_y)
    )
    partial_sums = jnp.einsum(
        "pxycqf,pmcxy->pfmq", shaped, tile.astype(jnp.float32), precision=lax.Precision.HIGHEST
    )
    partial_sums = partial_sums.reshape(ports_here * NF, MODES * 2)
    pieces = partial_sums.reshape(groups, owned, MODES * 2)
    result = jnp.sum(lax.all_to_all(pieces, ("gx", "gy"), 0, 0, tiled=False), axis=0)
    return (e_now, h_now, dft, result.reshape(owned, 1, MODES * 2))


def solution(mesh):
    return jax.shard_map(
        per_device,
        mesh=mesh,
        in_specs=(
            P(None, "gx", "gy", "gz"),
            P(None, "gx", "gy", "gz"),
            P("gx", "gy", "gz"),
            P("gz", "gx", "gy", None),
            P(),
            P("gz"),
            P("gz", None, None, None, None),
        ),
        out_specs=(
            P(None, "gx", "gy", "gz"),
            P(None, "gx", "gy", "gz"),
            P("gz", "gx", "gy", None),
            P(("gx", "gy"), "gz", None),
        ),
        check_vma=False,
    )
```

```python
import jax
import jax.numpy as jnp
from jax import lax
from jax.sharding import PartitionSpec as P

STEPS = 2
NF = 16
MODES = 2
HALO = 2
AXES = ("gx", "gy", "gz")


def shifted(value, axis, steps):
    count = lax.axis_size(axis)
    first, last = (max(0, -steps), min(count, count - steps))
    return lax.ppermute(value, axis, [(source, source + steps) for source in range(first, last)])


def widen(stack, dim, axis):
    count = stack.shape[dim]
    low = lax.slice_in_dim(stack, 0, HALO, axis=dim)
    high = lax.slice_in_dim(stack, count - HALO, count, axis=dim)
    from_below = shifted(high, axis, 1)
    from_above = shifted(low, axis, -1)
    return jnp.concatenate([from_below, stack, from_above], axis=dim)


def box(value, start, size):
    lead = value.ndim - 3
    return lax.slice(
        value,
        (0,) * lead + tuple(start),
        value.shape[:lead] + tuple(s + n for s, n in zip(start, size)),
    )


def moved(start, dim, step):
    return tuple(s + step if d == dim else s for d, s in enumerate(start))


def differ(value, start, size, dim, step):
    if step > 0:
        return box(value, moved(start, dim, 1), size) - box(value, start, size)
    return box(value, start, size) - box(value, moved(start, dim, -1), size)


def curl(field, start, size, step):
    vx, vy, vz = field[0], field[1], field[2]
    d = lambda v, dim: differ(v, start, size, dim, step)
    return jnp.stack([d(vz, 1) - d(vy, 2), d(vx, 2) - d(vz, 0), d(vy, 0) - d(vx, 1)])


def inside(origin, size, cells):
    masks = []
    for dim, axis in enumerate(AXES):
        count = lax.axis_size(axis)
        first = lax.axis_index(axis) * cells[dim] + origin
        where = first + jnp.arange(size[dim])
        masks.append((where >= 0) & (where < count * cells[dim]))
    return (
        masks[0][:, None, None] & masks[1][None, :, None] & masks[2][None, None, :]
    ).astype(jnp.float32)


def per_device(e_field, h_field, inv_permittivity, dft_sums, omega, port_z, mode_profiles):
    cells = e_field.shape[1:]
    cells_x, cells_y, cells_z = cells
    ports_here = dft_sums.shape[0]
    stack = jnp.concatenate([e_field, h_field, inv_permittivity[None]], axis=0)
    for dim, axis in enumerate(AXES):
        stack = widen(stack, dim + 1, axis)
    e0, h0, inv = stack[0:3], stack[3:6], stack[6]
    n = lambda k: tuple(c + k for c in cells)
    h1 = box(h0, (0, 0, 0), n(3)) - 0.5 * curl(e0, (0, 0, 0), n(3), 1)
    h1 = h1 * inside(-2, n(3), cells)
    e1 = box(e0, (1, 1, 1), n(2)) + 0.5 * box(inv, (1, 1, 1), n(2)) * curl(h1, (1, 1, 1), n(2), -1)
    h2 = box(h1, (1, 1, 1), n(1)) - 0.5 * curl(e1, (0, 0, 0), n(1), 1)
    h2 = h2 * inside(-1, n(1), cells)
    e2 = box(e1, (1, 1, 1), n(0)) + 0.5 * box(inv, (2, 2, 2), n(0)) * curl(h2, (1, 1, 1), n(0), -1)
    e1_here = box(e1, (1, 1, 1), n(0))
    h1_here = box(h1, (2, 2, 2), n(0))
    h2_here = box(h2, (1, 1, 1), n(0))
    local_z = port_z - lax.axis_index("gz") * cells_z
    select = (local_z[:, None] == jnp.arange(cells_z)[None, :]).astype(jnp.float32)
    dft = dft_sums
    for step, (e_now, h_now) in enumerate(((e1_here, h1_here), (e2, h2_here))):
        tangent = jnp.stack([e_now[0], e_now[1], h_now[0], h_now[1]])
        planes = jnp.einsum("cxyz,pz->pxyc", tangent, select, precision=lax.Precision.HIGHEST)
        phase = omega * jnp.float32(step + 1)
        trig = jnp.stack([jnp.cos(phase), jnp.sin(phase)])
        increment = planes[:, :, :, :, None, None] * trig[None, None, None, None, :, :]
        dft = dft + increment.reshape(dft.shape)
    shaped = dft.reshape(ports_here, cells_x, cells_y, 4, 2, NF)
    groups = lax.axis_size(("gx", "gy"))
    owned = ports_here * NF // groups
    start_x = lax.axis_index("gx") * cells_x
    start_y = lax.axis_index("gy") * cells_y
    tile = lax.dynamic_slice(
        mode_profiles, (0, 0, 0, start_x, start_y), (ports_here, MODES, 4, cells_x, cells_y)
    )
    partial_sums = jnp.einsum(
        "pxycqf,pmcxy->pfmq", shaped, tile.astype(jnp.float32), precision=lax.Precision.HIGHEST
    )
    partial_sums = partial_sums.reshape(ports_here * NF, MODES * 2)
    pieces = partial_sums.reshape(groups, owned, MODES * 2)
    result = jnp.sum(lax.all_to_all(pieces, ("gx", "gy"), 0, 0, tiled=False), axis=0)
    return (e2, h2_here, dft, result.reshape(owned, 1, MODES * 2))


def solution(mesh):
    return jax.shard_map(
        per_device,
        mesh=mesh,
        in_specs=(
            P(None, "gx", "gy", "gz"),
            P(None, "gx", "gy", "gz"),
            P("gx", "gy", "gz"),
            P("gz", "gx", "gy", None),
            P(),
            P("gz"),
            P("gz", None, None, None, None),
        ),
        out_specs=(
            P(None, "gx", "gy", "gz"),
            P(None, "gx", "gy", "gz"),
            P("gz", "gx", "gy", None),
            P(("gx", "gy"), "gz", None),
        ),
        check_vma=False,
    )
```

```python
import jax
import jax.numpy as jnp
from jax import lax
from jax.sharding import PartitionSpec as P

STEPS = 2
NF = 16
MODES = 2
HALO = 2
AXES = ("gx", "gy", "gz")


def shifted(value, axis, steps):
    count = lax.axis_size(axis)
    first, last = (max(0, -steps), min(count, count - steps))
    return lax.ppermute(value, axis, [(source, source + steps) for source in range(first, last)])


def widen(stack, dim, axis):
    count = stack.shape[dim]
    low = lax.slice_in_dim(stack, 0, HALO, axis=dim)
    high = lax.slice_in_dim(stack, count - HALO, count, axis=dim)
    from_below = shifted(high, axis, 1)
    from_above = shifted(low, axis, -1)
    return jnp.concatenate([from_below, stack, from_above], axis=dim)


def box(value, start, size):
    lead = value.ndim - 3
    return lax.slice(
        value,
        (0,) * lead + tuple(start),
        value.shape[:lead] + tuple(s + n for s, n in zip(start, size)),
    )


def moved(start, dim, step):
    return tuple(s + step if d == dim else s for d, s in enumerate(start))


def differ(value, start, size, dim, step):
    if step > 0:
        return box(value, moved(start, dim, 1), size) - box(value, start, size)
    return box(value, start, size) - box(value, moved(start, dim, -1), size)


def curl(field, start, size, step):
    vx, vy, vz = field[0], field[1], field[2]
    d = lambda v, dim: differ(v, start, size, dim, step)
    return jnp.stack([d(vz, 1) - d(vy, 2), d(vx, 2) - d(vz, 0), d(vy, 0) - d(vx, 1)])


def inside(origin, size, cells):
    masks = []
    for dim, axis in enumerate(AXES):
        count = lax.axis_size(axis)
        first = lax.axis_index(axis) * cells[dim] + origin
        where = first + jnp.arange(size[dim])
        masks.append((where >= 0) & (where < count * cells[dim]))
    return (
        masks[0][:, None, None] & masks[1][None, :, None] & masks[2][None, None, :]
    ).astype(jnp.float32)


def per_device(e_field, h_field, inv_permittivity, dft_sums, omega, port_z, mode_profiles):
    cells = e_field.shape[1:]
    cells_x, cells_y, cells_z = cells
    ports_here = dft_sums.shape[0]
    stack = jnp.concatenate([e_field, h_field, inv_permittivity[None]], axis=0)
    for dim, axis in enumerate(AXES):
        stack = widen(stack, dim + 1, axis)
    e0, h0, inv = stack[0:3], stack[3:6], stack[6]
    n = lambda k: tuple(c + k for c in cells)
    h1 = box(h0, (0, 0, 0), n(3)) - 0.5 * curl(e0, (0, 0, 0), n(3), 1)
    h1 = h1 * inside(-2, n(3), cells)
    e1 = box(e0, (1, 1, 1), n(2)) + 0.5 * box(inv, (1, 1, 1), n(2)) * curl(h1, (1, 1, 1), n(2), -1)
    h2 = box(h1, (1, 1, 1), n(1)) - 0.5 * curl(e1, (0, 0, 0), n(1), 1)
    h2 = h2 * inside(-1, n(1), cells)
    e2 = box(e1, (1, 1, 1), n(0)) + 0.5 * box(inv, (2, 2, 2), n(0)) * curl(h2, (1, 1, 1), n(0), -1)
    e1_here = box(e1, (1, 1, 1), n(0))
    h1_here = box(h1, (2, 2, 2), n(0))
    h2_here = box(h2, (1, 1, 1), n(0))
    local_z = port_z - lax.axis_index("gz") * cells_z
    onehot = (local_z[:, None] == jnp.arange(cells_z)[None, :]).astype(jnp.float32)
    lanes = dft_sums.shape[-1]
    lane_part = jnp.arange(lanes) // (lanes // 4)
    spread_of = (lane_part[None, :] == jnp.arange(4)[:, None]).astype(jnp.float32)
    dft = dft_sums
    for step, (e_now, h_now) in enumerate(((e1_here, h1_here), (e2, h2_here))):
        tangent = jnp.stack([e_now[0], e_now[1], h_now[0], h_now[1]])
        planes = jnp.sum(tangent[None] * onehot[:, None, None, None, :], axis=-1)
        phase = omega * jnp.float32(step + 1)
        trig = jnp.stack([jnp.cos(phase), jnp.sin(phase)])
        coef = jnp.tile(trig.reshape(-1), 4)
        spread = jnp.sum(planes[..., None] * spread_of[None, :, None, None, :], axis=1)
        dft = dft + spread * coef
    groups = lax.axis_size(("gx", "gy"))
    owned = ports_here * NF // groups
    start_x = lax.axis_index("gx") * cells_x
    start_y = lax.axis_index("gy") * cells_y
    tile = lax.dynamic_slice(
        mode_profiles, (0, 0, 0, start_x, start_y), (ports_here, MODES, 4, cells_x, cells_y)
    )
    weights = tile.reshape(ports_here, MODES * 4, cells_x, cells_y).astype(jnp.float32)
    crossed = jnp.einsum("pxyl,pnxy->pnl", dft, weights, precision=lax.Precision.HIGHEST)
    crossed = crossed.reshape(ports_here, MODES, 4, 4, 2, NF)
    diagonal = sum(crossed[:, :, c, c] for c in range(4))
    partial_sums = jnp.transpose(diagonal, (0, 3, 1, 2)).reshape(ports_here * NF, MODES * 2)
    pieces = partial_sums.reshape(groups, owned, MODES * 2)
    result = jnp.sum(lax.all_to_all(pieces, ("gx", "gy"), 0, 0, tiled=False), axis=0)
    return (e2, h2_here, dft, result.reshape(owned, 1, MODES * 2))


def solution(mesh):
    return jax.shard_map(
        per_device,
        mesh=mesh,
        in_specs=(
            P(None, "gx", "gy", "gz"),
            P(None, "gx", "gy", "gz"),
            P("gx", "gy", "gz"),
            P("gz", "gx", "gy", None),
            P(),
            P("gz"),
            P("gz", None, None, None, None),
        ),
        out_specs=(
            P(None, "gx", "gy", "gz"),
            P(None, "gx", "gy", "gz"),
            P("gz", "gx", "gy", None),
            P(("gx", "gy"), "gz", None),
        ),
        check_vma=False,
    )
```

```python
import jax
import jax.numpy as jnp
from jax import lax
from jax.sharding import PartitionSpec as P
from jax.experimental.layout import Layout, with_layout_constraint

STEPS = 2
NF = 16
MODES = 2
HALO = 2
AXES = ("gx", "gy", "gz")


def pin(value):
    return with_layout_constraint(value, Layout(tuple(range(value.ndim))))


def shifted(value, axis, steps):
    count = lax.axis_size(axis)
    first, last = (max(0, -steps), min(count, count - steps))
    return lax.ppermute(value, axis, [(source, source + steps) for source in range(first, last)])


def widen(stack, dim, axis):
    count = stack.shape[dim]
    low = lax.slice_in_dim(stack, 0, HALO, axis=dim)
    high = lax.slice_in_dim(stack, count - HALO, count, axis=dim)
    from_below = shifted(high, axis, 1)
    from_above = shifted(low, axis, -1)
    return jnp.concatenate([from_below, stack, from_above], axis=dim)


def box(value, start, size):
    lead = value.ndim - 3
    return lax.slice(
        value,
        (0,) * lead + tuple(start),
        value.shape[:lead] + tuple(s + n for s, n in zip(start, size)),
    )


def moved(start, dim, step):
    return tuple(s + step if d == dim else s for d, s in enumerate(start))


def differ(value, start, size, dim, step):
    if step > 0:
        return box(value, moved(start, dim, 1), size) - box(value, start, size)
    return box(value, start, size) - box(value, moved(start, dim, -1), size)


def curl(field, start, size, step):
    vx, vy, vz = field[0], field[1], field[2]
    d = lambda v, dim: differ(v, start, size, dim, step)
    return jnp.stack([d(vz, 1) - d(vy, 2), d(vx, 2) - d(vz, 0), d(vy, 0) - d(vx, 1)])


def inside(origin, size, cells):
    masks = []
    for dim, axis in enumerate(AXES):
        count = lax.axis_size(axis)
        first = lax.axis_index(axis) * cells[dim] + origin
        where = first + jnp.arange(size[dim])
        masks.append((where >= 0) & (where < count * cells[dim]))
    return (
        masks[0][:, None, None] & masks[1][None, :, None] & masks[2][None, None, :]
    ).astype(jnp.float32)


def per_device(e_field, h_field, inv_permittivity, dft_sums, omega, port_z, mode_profiles):
    cells = e_field.shape[1:]
    cells_x, cells_y, cells_z = cells
    ports_here = dft_sums.shape[0]
    stack = jnp.concatenate([e_field, h_field, inv_permittivity[None]], axis=0)
    for dim, axis in enumerate(AXES):
        stack = pin(widen(stack, dim + 1, axis))
    e0, h0, inv = stack[0:3], stack[3:6], stack[6]
    n = lambda k: tuple(c + k for c in cells)
    h1 = box(h0, (0, 0, 0), n(3)) - 0.5 * curl(e0, (0, 0, 0), n(3), 1)
    h1 = pin(h1 * inside(-2, n(3), cells))
    e1 = pin(box(e0, (1, 1, 1), n(2)) + 0.5 * box(inv, (1, 1, 1), n(2)) * curl(h1, (1, 1, 1), n(2), -1))
    h2 = box(h1, (1, 1, 1), n(1)) - 0.5 * curl(e1, (0, 0, 0), n(1), 1)
    h2 = pin(h2 * inside(-1, n(1), cells))
    e2 = pin(box(e1, (1, 1, 1), n(0)) + 0.5 * box(inv, (2, 2, 2), n(0)) * curl(h2, (1, 1, 1), n(0), -1))
    e1_here = box(e1, (1, 1, 1), n(0))
    h1_here = box(h1, (2, 2, 2), n(0))
    h2_here = box(h2, (1, 1, 1), n(0))
    local_z = port_z - lax.axis_index("gz") * cells_z
    onehot = (local_z[:, None] == jnp.arange(cells_z)[None, :]).astype(jnp.float32)
    lanes = dft_sums.shape[-1]
    lane_part = jnp.arange(lanes) // (lanes // 4)
    spread_of = (lane_part[None, :] == jnp.arange(4)[:, None]).astype(jnp.float32)
    dft = dft_sums
    for step, (e_now, h_now) in enumerate(((e1_here, h1_here), (e2, h2_here))):
        tangent = pin(jnp.stack([e_now[0], e_now[1], h_now[0], h_now[1]]))
        planes = jnp.sum(tangent[None] * onehot[:, None, None, None, :], axis=-1)
        phase = omega * jnp.float32(step + 1)
        trig = jnp.stack([jnp.cos(phase), jnp.sin(phase)])
        coef = jnp.tile(trig.reshape(-1), 4)
        spread = jnp.sum(planes[..., None] * spread_of[None, :, None, None, :], axis=1)
        dft = pin(dft + spread * coef)
    groups = lax.axis_size(("gx", "gy"))
    owned = ports_here * NF // groups
    start_x = lax.axis_index("gx") * cells_x
    start_y = lax.axis_index("gy") * cells_y
    tile = lax.dynamic_slice(
        mode_profiles, (0, 0, 0, start_x, start_y), (ports_here, MODES, 4, cells_x, cells_y)
    )
    weights = tile.reshape(ports_here, MODES * 4, cells_x, cells_y).astype(jnp.float32)
    crossed = jnp.einsum("pxyl,pnxy->pnl", dft, weights, precision=lax.Precision.HIGHEST)
    crossed = crossed.reshape(ports_here, MODES, 4, 4, 2, NF)
    diagonal = sum(crossed[:, :, c, c] for c in range(4))
    partial_sums = jnp.transpose(diagonal, (0, 3, 1, 2)).reshape(ports_here * NF, MODES * 2)
    pieces = partial_sums.reshape(groups, owned, MODES * 2)
    result = jnp.sum(lax.all_to_all(pieces, ("gx", "gy"), 0, 0, tiled=False), axis=0)
    return (e2, h2_here, dft, result.reshape(owned, 1, MODES * 2))


def solution(mesh):
    return jax.shard_map(
        per_device,
        mesh=mesh,
        in_specs=(
            P(None, "gx", "gy", "gz"),
            P(None, "gx", "gy", "gz"),
            P("gx", "gy", "gz"),
            P("gz", "gx", "gy", None),
            P(),
            P("gz"),
            P("gz", None, None, None, None),
        ),
        out_specs=(
            P(None, "gx", "gy", "gz"),
            P(None, "gx", "gy", "gz"),
            P("gz", "gx", "gy", None),
            P(("gx", "gy"), "gz", None),
        ),
        check_vma=False,
    )
```

```python
import jax
import jax.numpy as jnp
from jax import lax
from jax.sharding import PartitionSpec as P
from jax.experimental.layout import Layout, with_layout_constraint

STEPS = 2
NF = 16
MODES = 2
HALO = 2
AXES = ("gx", "gy", "gz")


def pin(value):
    return with_layout_constraint(value, Layout(tuple(range(value.ndim))))


def shifted(value, axis, steps):
    count = lax.axis_size(axis)
    first, last = (max(0, -steps), min(count, count - steps))
    return lax.ppermute(value, axis, [(source, source + steps) for source in range(first, last)])


def widen(stack, dim, axis, cyclic):
    count = stack.shape[dim]
    low = lax.slice_in_dim(stack, 0, HALO, axis=dim)
    high = lax.slice_in_dim(stack, count - HALO, count, axis=dim)
    from_below = shifted(high, axis, 1)
    from_above = shifted(low, axis, -1)
    if cyclic:
        return jnp.concatenate([stack, from_above, from_below], axis=dim)
    return jnp.concatenate([from_below, stack, from_above], axis=dim)


def rows(value, start, size):
    return lax.slice_in_dim(value, start, start + size, axis=value.ndim - 3)


def differ(value, start, size, dim, step):
    here = rows(value, start, size)
    if dim == 0:
        return rows(value, start + step, size) - here if step > 0 else here - rows(value, start - 1, size)
    axis = value.ndim - 3 + dim
    return jnp.roll(here, -1, axis=axis) - here if step > 0 else here - jnp.roll(here, 1, axis=axis)


def curl(field, start, size, step):
    vx, vy, vz = field[0], field[1], field[2]
    d = lambda v, dim: differ(v, start, size, dim, step)
    return jnp.stack([d(vz, 1) - d(vy, 2), d(vx, 2) - d(vz, 0), d(vy, 0) - d(vx, 1)])


def cyclic_cells(count):
    return jnp.concatenate([jnp.arange(count + HALO), jnp.arange(-HALO, 0)])


def inside(origin, size, cells):
    where = [origin + jnp.arange(size), cyclic_cells(cells[1]), cyclic_cells(cells[2])]
    masks = []
    for dim, axis in enumerate(AXES):
        first = lax.axis_index(axis) * cells[dim] + where[dim]
        masks.append((first >= 0) & (first < lax.axis_size(axis) * cells[dim]))
    return (
        masks[0][:, None, None] & masks[1][None, :, None] & masks[2][None, None, :]
    ).astype(jnp.float32)


def per_device(e_field, h_field, inv_permittivity, dft_sums, omega, port_z, mode_profiles):
    cells = e_field.shape[1:]
    cells_x, cells_y, cells_z = cells
    ports_here = dft_sums.shape[0]
    stack = jnp.concatenate([e_field, h_field, inv_permittivity[None]], axis=0)
    for dim in (2, 1, 0):
        stack = pin(widen(stack, dim + 1, AXES[dim], dim > 0))
    e0, h0, inv = stack[0:3], stack[3:6], stack[6]
    h1 = rows(h0, 0, cells_x + 3) - 0.5 * curl(e0, 0, cells_x + 3, 1)
    h1 = pin(h1 * inside(-2, cells_x + 3, cells))
    e1 = pin(rows(e0, 1, cells_x + 2) + 0.5 * rows(inv, 1, cells_x + 2) * curl(h1, 1, cells_x + 2, -1))
    h2 = rows(h1, 1, cells_x + 1) - 0.5 * curl(e1, 0, cells_x + 1, 1)
    h2 = pin(h2 * inside(-1, cells_x + 1, cells))
    e2 = pin(rows(e1, 1, cells_x) + 0.5 * rows(inv, 2, cells_x) * curl(h2, 1, cells_x, -1))
    block = lambda v: v[..., :cells_y, :cells_z]
    e1_here = block(rows(e1, 1, cells_x))
    h1_here = block(rows(h1, 2, cells_x))
    e2 = block(e2)
    h2_here = block(rows(h2, 1, cells_x))
    local_z = port_z - lax.axis_index("gz") * cells_z
    onehot = (local_z[:, None] == jnp.arange(cells_z)[None, :]).astype(jnp.float32)
    lanes = dft_sums.shape[-1]
    lane_part = jnp.arange(lanes) // (lanes // 4)
    spread_of = (lane_part[None, :] == jnp.arange(4)[:, None]).astype(jnp.float32)
    dft = dft_sums
    for step, (e_now, h_now) in enumerate(((e1_here, h1_here), (e2, h2_here))):
        tangent = pin(jnp.stack([e_now[0], e_now[1], h_now[0], h_now[1]]))
        planes = jnp.sum(tangent[None] * onehot[:, None, None, None, :], axis=-1)
        phase = omega * jnp.float32(step + 1)
        trig = jnp.stack([jnp.cos(phase), jnp.sin(phase)])
        coef = jnp.tile(trig.reshape(-1), 4)
        spread = jnp.sum(planes[..., None] * spread_of[None, :, None, None, :], axis=1)
        dft = pin(dft + spread * coef)
    groups = lax.axis_size(("gx", "gy"))
    owned = ports_here * NF // groups
    start_x = lax.axis_index("gx") * cells_x
    start_y = lax.axis_index("gy") * cells_y
    tile = lax.dynamic_slice(
        mode_profiles, (0, 0, 0, start_x, start_y), (ports_here, MODES, 4, cells_x, cells_y)
    )
    weights = tile.reshape(ports_here, MODES * 4, cells_x, cells_y).astype(jnp.float32)
    crossed = jnp.einsum("pxyl,pnxy->pnl", dft, weights, precision=lax.Precision.HIGHEST)
    crossed = crossed.reshape(ports_here, MODES, 4, 4, 2, NF)
    diagonal = sum(crossed[:, :, c, c] for c in range(4))
    partial_sums = jnp.transpose(diagonal, (0, 3, 1, 2)).reshape(ports_here * NF, MODES * 2)
    pieces = partial_sums.reshape(groups, owned, MODES * 2)
    result = jnp.sum(lax.all_to_all(pieces, ("gx", "gy"), 0, 0, tiled=False), axis=0)
    return (e2, h2_here, dft, result.reshape(owned, 1, MODES * 2))


def solution(mesh):
    return jax.shard_map(
        per_device,
        mesh=mesh,
        in_specs=(
            P(None, "gx", "gy", "gz"),
            P(None, "gx", "gy", "gz"),
            P("gx", "gy", "gz"),
            P("gz", "gx", "gy", None),
            P(),
            P("gz"),
            P("gz", None, None, None, None),
        ),
        out_specs=(
            P(None, "gx", "gy", "gz"),
            P(None, "gx", "gy", "gz"),
            P("gz", "gx", "gy", None),
            P(("gx", "gy"), "gz", None),
        ),
        check_vma=False,
    )
```

```python
import jax
import jax.numpy as jnp
from jax import lax
from jax.sharding import PartitionSpec as P
from jax.experimental.layout import Layout, with_layout_constraint

STEPS = 2
NF = 16
MODES = 2
HALO = 2
AXES = ("gx", "gy", "gz")


def pin(value):
    return with_layout_constraint(value, Layout(tuple(range(value.ndim))))


def shifted(value, axis, steps):
    count = lax.axis_size(axis)
    first, last = (max(0, -steps), min(count, count - steps))
    return lax.ppermute(value, axis, [(source, source + steps) for source in range(first, last)])


def widen(stack, dim, axis):
    count = stack.shape[dim]
    low = lax.slice_in_dim(stack, 0, HALO, axis=dim)
    high = lax.slice_in_dim(stack, count - HALO, count, axis=dim)
    from_below = shifted(high, axis, 1)
    from_above = shifted(low, axis, -1)
    return jnp.concatenate([from_below, stack, from_above], axis=dim)


def widen_lanes(stack, axis):
    lanes = stack.shape[-1]
    flat = stack.reshape(-1, lanes)
    lane = jnp.arange(lanes)
    edges = jnp.concatenate([jnp.arange(HALO), jnp.arange(lanes - HALO, lanes)])
    pick = (lane[None, :] == edges[:, None]).astype(jnp.float32)
    faces = jnp.einsum("kz,rz->kr", pick, flat, precision=lax.Precision.HIGHEST)
    from_above = shifted(faces[:HALO], axis, -1)
    from_below = shifted(faces[HALO:], axis, 1)
    ghosts = jnp.concatenate([from_below, from_above], axis=0)
    out = jnp.arange(lanes + 2 * HALO)
    spots = jnp.concatenate([jnp.arange(HALO), jnp.arange(lanes + HALO, lanes + 2 * HALO)])
    move = (out[None, :] == lane[:, None] + HALO).astype(jnp.float32)
    place = (out[None, :] == spots[:, None]).astype(jnp.float32)
    wide = jnp.dot(flat, move, precision=lax.Precision.HIGHEST) + jnp.einsum(
        "kr,kl->rl", ghosts, place, precision=lax.Precision.HIGHEST
    )
    return wide.reshape(stack.shape[:-1] + (lanes + 2 * HALO,))


def box(value, start, size):
    lead = value.ndim - 3
    return lax.slice(
        value,
        (0,) * lead + tuple(start),
        value.shape[:lead] + tuple(s + n for s, n in zip(start, size)),
    )


def moved(start, dim, step):
    return tuple(s + step if d == dim else s for d, s in enumerate(start))


def differ(value, start, size, dim, step):
    if step > 0:
        return box(value, moved(start, dim, 1), size) - box(value, start, size)
    return box(value, start, size) - box(value, moved(start, dim, -1), size)


def curl(field, start, size, step):
    vx, vy, vz = field[0], field[1], field[2]
    d = lambda v, dim: differ(v, start, size, dim, step)
    return jnp.stack([d(vz, 1) - d(vy, 2), d(vx, 2) - d(vz, 0), d(vy, 0) - d(vx, 1)])


def inside(origin, size, cells):
    masks = []
    for dim, axis in enumerate(AXES):
        count = lax.axis_size(axis)
        first = lax.axis_index(axis) * cells[dim] + origin
        where = first + jnp.arange(size[dim])
        masks.append((where >= 0) & (where < count * cells[dim]))
    return (
        masks[0][:, None, None] & masks[1][None, :, None] & masks[2][None, None, :]
    ).astype(jnp.float32)


def per_device(e_field, h_field, inv_permittivity, dft_sums, omega, port_z, mode_profiles):
    cells = e_field.shape[1:]
    cells_x, cells_y, cells_z = cells
    ports_here = dft_sums.shape[0]
    stack = jnp.concatenate([e_field, h_field, inv_permittivity[None]], axis=0)
    stack = pin(widen(stack, 1, "gx"))
    stack = widen(stack, 2, "gy")
    spare = -stack.shape[2] % 8
    stack = pin(jnp.pad(stack, ((0, 0), (0, 0), (0, spare), (0, 0))))
    stack = pin(widen_lanes(stack, "gz"))
    e0, h0, inv = stack[0:3], stack[3:6], stack[6]
    n = lambda k: tuple(c + k for c in cells)
    h1 = box(h0, (0, 0, 0), n(3)) - 0.5 * curl(e0, (0, 0, 0), n(3), 1)
    h1 = pin(h1 * inside(-2, n(3), cells))
    e1 = pin(box(e0, (1, 1, 1), n(2)) + 0.5 * box(inv, (1, 1, 1), n(2)) * curl(h1, (1, 1, 1), n(2), -1))
    h2 = box(h1, (1, 1, 1), n(1)) - 0.5 * curl(e1, (0, 0, 0), n(1), 1)
    h2 = pin(h2 * inside(-1, n(1), cells))
    e2 = pin(box(e1, (1, 1, 1), n(0)) + 0.5 * box(inv, (2, 2, 2), n(0)) * curl(h2, (1, 1, 1), n(0), -1))
    e1_here = box(e1, (1, 1, 1), n(0))
    h1_here = box(h1, (2, 2, 2), n(0))
    h2_here = box(h2, (1, 1, 1), n(0))
    local_z = port_z - lax.axis_index("gz") * cells_z
    onehot = (local_z[:, None] == jnp.arange(cells_z)[None, :]).astype(jnp.float32)
    lanes = dft_sums.shape[-1]
    lane_part = jnp.arange(lanes) // (lanes // 4)
    spread_of = (lane_part[None, :] == jnp.arange(4)[:, None]).astype(jnp.float32)
    dft = dft_sums
    for step, (e_now, h_now) in enumerate(((e1_here, h1_here), (e2, h2_here))):
        tangent = pin(jnp.stack([e_now[0], e_now[1], h_now[0], h_now[1]]))
        planes = jnp.sum(tangent[None] * onehot[:, None, None, None, :], axis=-1)
        phase = omega * jnp.float32(step + 1)
        trig = jnp.stack([jnp.cos(phase), jnp.sin(phase)])
        coef = jnp.tile(trig.reshape(-1), 4)
        spread = jnp.sum(planes[..., None] * spread_of[None, :, None, None, :], axis=1)
        dft = pin(dft + spread * coef)
    groups = lax.axis_size(("gx", "gy"))
    owned = ports_here * NF // groups
    start_x = lax.axis_index("gx") * cells_x
    start_y = lax.axis_index("gy") * cells_y
    tile = lax.dynamic_slice(
        mode_profiles, (0, 0, 0, start_x, start_y), (ports_here, MODES, 4, cells_x, cells_y)
    )
    weights = tile.reshape(ports_here, MODES * 4, cells_x, cells_y).astype(jnp.float32)
    crossed = jnp.einsum("pxyl,pnxy->pnl", dft, weights, precision=lax.Precision.HIGHEST)
    crossed = crossed.reshape(ports_here, MODES, 4, 4, 2, NF)
    diagonal = sum(crossed[:, :, c, c] for c in range(4))
    partial_sums = jnp.transpose(diagonal, (0, 3, 1, 2)).reshape(ports_here * NF, MODES * 2)
    pieces = partial_sums.reshape(groups, owned, MODES * 2)
    result = jnp.sum(lax.all_to_all(pieces, ("gx", "gy"), 0, 0, tiled=False), axis=0)
    return (e2, h2_here, dft, result.reshape(owned, 1, MODES * 2))


def solution(mesh):
    return jax.shard_map(
        per_device,
        mesh=mesh,
        in_specs=(
            P(None, "gx", "gy", "gz"),
            P(None, "gx", "gy", "gz"),
            P("gx", "gy", "gz"),
            P("gz", "gx", "gy", None),
            P(),
            P("gz"),
            P("gz", None, None, None, None),
        ),
        out_specs=(
            P(None, "gx", "gy", "gz"),
            P(None, "gx", "gy", "gz"),
            P("gz", "gx", "gy", None),
            P(("gx", "gy"), "gz", None),
        ),
        check_vma=False,
    )
```

```python
import jax
import jax.numpy as jnp
from jax import lax
from jax.sharding import PartitionSpec as P
from jax.experimental.layout import Layout, with_layout_constraint

STEPS = 2
NF = 16
MODES = 2
HALO = 2
AXES = ("gx", "gy", "gz")


def pin(value):
    return with_layout_constraint(value, Layout(tuple(range(value.ndim))))


def shifted(value, axis, steps):
    count = lax.axis_size(axis)
    first, last = (max(0, -steps), min(count, count - steps))
    return lax.ppermute(value, axis, [(source, source + steps) for source in range(first, last)])


def widen(stack, dim, axis):
    count = stack.shape[dim]
    low = lax.slice_in_dim(stack, 0, HALO, axis=dim)
    high = lax.slice_in_dim(stack, count - HALO, count, axis=dim)
    from_below = shifted(high, axis, 1)
    from_above = shifted(low, axis, -1)
    return jnp.concatenate([from_below, stack, from_above], axis=dim)


def widen_lanes(stack, axis):
    lanes = stack.shape[-1]
    flat = stack.reshape(-1, lanes)
    lane = jnp.arange(lanes)
    edges = jnp.concatenate([jnp.arange(HALO), jnp.arange(lanes - HALO, lanes)])
    pick = (lane[None, :] == edges[:, None]).astype(jnp.float32)
    faces = jnp.einsum("kz,rz->kr", pick, flat, precision=lax.Precision.HIGHEST)
    from_above = shifted(faces[:HALO], axis, -1)
    from_below = shifted(faces[HALO:], axis, 1)
    ghosts = jnp.concatenate([from_below, from_above], axis=0)
    out = jnp.arange(lanes + 2 * HALO)
    spots = jnp.concatenate([jnp.arange(HALO), jnp.arange(lanes + HALO, lanes + 2 * HALO)])
    move = (out[None, :] == lane[:, None] + HALO).astype(jnp.float32)
    place = (out[None, :] == spots[:, None]).astype(jnp.float32)
    wide = jnp.dot(flat, move, precision=lax.Precision.HIGHEST) + jnp.einsum(
        "kr,kl->rl", ghosts, place, precision=lax.Precision.HIGHEST
    )
    return wide.reshape(stack.shape[:-1] + (lanes + 2 * HALO,))


def box(value, start, size):
    lead = value.ndim - 3
    return lax.slice(
        value,
        (0,) * lead + tuple(start),
        value.shape[:lead] + tuple(s + n for s, n in zip(start, size)),
    )


def moved(start, dim, step):
    return tuple(s + step if d == dim else s for d, s in enumerate(start))


def differ(value, start, size, dim, step):
    if step > 0:
        return box(value, moved(start, dim, 1), size) - box(value, start, size)
    return box(value, start, size) - box(value, moved(start, dim, -1), size)


def curl(field, start, size, step):
    vx, vy, vz = field[0], field[1], field[2]
    d = lambda v, dim: differ(v, start, size, dim, step)
    return jnp.stack([d(vz, 1) - d(vy, 2), d(vx, 2) - d(vz, 0), d(vy, 0) - d(vx, 1)])


def inside(origin, size, cells):
    masks = []
    for dim, axis in enumerate(AXES):
        count = lax.axis_size(axis)
        first = lax.axis_index(axis) * cells[dim] + origin
        where = first + jnp.arange(size[dim])
        masks.append((where >= 0) & (where < count * cells[dim]))
    return (
        masks[0][:, None, None] & masks[1][None, :, None] & masks[2][None, None, :]
    ).astype(jnp.float32)


def per_device(e_field, h_field, inv_permittivity, dft_sums, omega, port_z, mode_profiles):
    cells = e_field.shape[1:]
    cells_x, cells_y, cells_z = cells
    ports_here = dft_sums.shape[0]
    stack = jnp.concatenate([e_field, h_field, inv_permittivity[None]], axis=0)
    stack = pin(widen(stack, 1, "gx"))
    stack = widen(stack, 2, "gy")
    spare = -stack.shape[2] % 8
    stack = pin(jnp.pad(stack, ((0, 0), (0, 0), (0, spare), (0, 0))))
    stack = pin(widen_lanes(stack, "gz"))
    e0, h0, inv = stack[0:3], stack[3:6], stack[6]
    n = lambda k: tuple(c + k for c in cells)
    h1 = box(h0, (0, 0, 0), n(3)) - 0.5 * curl(e0, (0, 0, 0), n(3), 1)
    h1 = pin(h1 * inside(-2, n(3), cells))
    e1 = pin(box(e0, (1, 1, 1), n(2)) + 0.5 * box(inv, (1, 1, 1), n(2)) * curl(h1, (1, 1, 1), n(2), -1))
    h2 = box(h1, (1, 1, 1), n(1)) - 0.5 * curl(e1, (0, 0, 0), n(1), 1)
    h2 = pin(h2 * inside(-1, n(1), cells))
    e2 = pin(box(e1, (1, 1, 1), n(0)) + 0.5 * box(inv, (2, 2, 2), n(0)) * curl(h2, (1, 1, 1), n(0), -1))
    e1_here = box(e1, (1, 1, 1), n(0))
    h1_here = box(h1, (2, 2, 2), n(0))
    h2_here = box(h2, (1, 1, 1), n(0))
    local_z = port_z - lax.axis_index("gz") * cells_z
    onehot = (local_z[:, None] == jnp.arange(cells_z)[None, :]).astype(jnp.float32)
    lanes = dft_sums.shape[-1]
    lane_part = jnp.arange(lanes) // (lanes // 4)
    spread_of = (lane_part[None, :] == jnp.arange(4)[:, None]).astype(jnp.float32)
    dft = dft_sums
    at = lambda value: jnp.sum(value[None] * onehot[:, None, None, :], axis=-1)
    near = lambda v, x, y, z: at(box(v, (x, y, z), cells))
    h2x, h2y, h2z = h2[0], h2[1], h2[2]
    half_inv = 0.5 * near(inv, 2, 2, 2)
    e2x = near(e1[0], 1, 1, 1) + half_inv * (
        (near(h2z, 1, 1, 1) - near(h2z, 1, 0, 1)) - (near(h2y, 1, 1, 1) - near(h2y, 1, 1, 0))
    )
    e2y = near(e1[1], 1, 1, 1) + half_inv * (
        (near(h2x, 1, 1, 1) - near(h2x, 1, 1, 0)) - (near(h2z, 1, 1, 1) - near(h2z, 0, 1, 1))
    )
    ported = jnp.stack([e2x, e2y, near(h2x, 1, 1, 1), near(h2y, 1, 1, 1)], axis=1)
    for step, (e_now, h_now) in enumerate(((e1_here, h1_here), (None, None))):
        if e_now is None:
            planes = ported
        else:
            tangent = pin(jnp.stack([e_now[0], e_now[1], h_now[0], h_now[1]]))
            planes = jnp.sum(tangent[None] * onehot[:, None, None, None, :], axis=-1)
        phase = omega * jnp.float32(step + 1)
        trig = jnp.stack([jnp.cos(phase), jnp.sin(phase)])
        coef = jnp.tile(trig.reshape(-1), 4)
        spread = jnp.sum(planes[..., None] * spread_of[None, :, None, None, :], axis=1)
        dft = pin(dft + spread * coef)
    groups = lax.axis_size(("gx", "gy"))
    owned = ports_here * NF // groups
    start_x = lax.axis_index("gx") * cells_x
    start_y = lax.axis_index("gy") * cells_y
    tile = lax.dynamic_slice(
        mode_profiles, (0, 0, 0, start_x, start_y), (ports_here, MODES, 4, cells_x, cells_y)
    )
    weights = tile.reshape(ports_here, MODES * 4, cells_x, cells_y).astype(jnp.float32)
    crossed = jnp.einsum("pxyl,pnxy->pnl", dft, weights, precision=lax.Precision.HIGHEST)
    crossed = crossed.reshape(ports_here, MODES, 4, 4, 2, NF)
    diagonal = sum(crossed[:, :, c, c] for c in range(4))
    partial_sums = jnp.transpose(diagonal, (0, 3, 1, 2)).reshape(ports_here * NF, MODES * 2)
    pieces = partial_sums.reshape(groups, owned, MODES * 2)
    result = jnp.sum(lax.all_to_all(pieces, ("gx", "gy"), 0, 0, tiled=False), axis=0)
    return (e2, h2_here, dft, result.reshape(owned, 1, MODES * 2))


def solution(mesh):
    return jax.shard_map(
        per_device,
        mesh=mesh,
        in_specs=(
            P(None, "gx", "gy", "gz"),
            P(None, "gx", "gy", "gz"),
            P("gx", "gy", "gz"),
            P("gz", "gx", "gy", None),
            P(),
            P("gz"),
            P("gz", None, None, None, None),
        ),
        out_specs=(
            P(None, "gx", "gy", "gz"),
            P(None, "gx", "gy", "gz"),
            P("gz", "gx", "gy", None),
            P(("gx", "gy"), "gz", None),
        ),
        check_vma=False,
    )
```

```python
import jax
import jax.numpy as jnp
from jax import lax
from jax.sharding import PartitionSpec as P
from jax.experimental.layout import Layout, with_layout_constraint
from jax.experimental import pallas as pl
from jax.experimental.pallas import tpu as pltpu

STEPS = 2
NF = 16
MODES = 2
HALO = 2
AXES = ("gx", "gy", "gz")


def pin(value):
    return with_layout_constraint(value, Layout(tuple(range(value.ndim))))


def shifted(value, axis, steps):
    count = lax.axis_size(axis)
    first, last = (max(0, -steps), min(count, count - steps))
    return lax.ppermute(value, axis, [(source, source + steps) for source in range(first, last)])


def widen(stack, dim, axis):
    count = stack.shape[dim]
    low = lax.slice_in_dim(stack, 0, HALO, axis=dim)
    high = lax.slice_in_dim(stack, count - HALO, count, axis=dim)
    from_below = shifted(high, axis, 1)
    from_above = shifted(low, axis, -1)
    return jnp.concatenate([from_below, stack, from_above], axis=dim)


def widen_lanes(stack, axis):
    lanes = stack.shape[-1]
    flat = stack.reshape(-1, lanes)
    lane = jnp.arange(lanes)
    edges = jnp.concatenate([jnp.arange(HALO), jnp.arange(lanes - HALO, lanes)])
    pick = (lane[None, :] == edges[:, None]).astype(jnp.float32)
    faces = jnp.einsum("kz,rz->kr", pick, flat, precision=lax.Precision.HIGHEST)
    from_above = shifted(faces[:HALO], axis, -1)
    from_below = shifted(faces[HALO:], axis, 1)
    ghosts = jnp.concatenate([from_below, from_above], axis=0)
    out = jnp.arange(lanes + 2 * HALO)
    spots = jnp.concatenate([jnp.arange(HALO), jnp.arange(lanes + HALO, lanes + 2 * HALO)])
    move = (out[None, :] == lane[:, None] + HALO).astype(jnp.float32)
    place = (out[None, :] == spots[:, None]).astype(jnp.float32)
    wide = jnp.dot(flat, move, precision=lax.Precision.HIGHEST) + jnp.einsum(
        "kr,kl->rl", ghosts, place, precision=lax.Precision.HIGHEST
    )
    return wide.reshape(stack.shape[:-1] + (lanes + 2 * HALO,))


def box(value, start, size):
    lead = value.ndim - 3
    return lax.slice(
        value,
        (0,) * lead + tuple(start),
        value.shape[:lead] + tuple(s + n for s, n in zip(start, size)),
    )


def moved(start, dim, step):
    return tuple(s + step if d == dim else s for d, s in enumerate(start))


def differ(value, start, size, dim, step):
    if step > 0:
        return box(value, moved(start, dim, 1), size) - box(value, start, size)
    return box(value, start, size) - box(value, moved(start, dim, -1), size)


def curl(field, start, size, step):
    vx, vy, vz = field[0], field[1], field[2]
    d = lambda v, dim: differ(v, start, size, dim, step)
    return jnp.stack([d(vz, 1) - d(vy, 2), d(vx, 2) - d(vz, 0), d(vy, 0) - d(vx, 1)])


def inside(origin, size, cells):
    masks = []
    for dim, axis in enumerate(AXES):
        count = lax.axis_size(axis)
        first = lax.axis_index(axis) * cells[dim] + origin
        where = first + jnp.arange(size[dim])
        masks.append((where >= 0) & (where < count * cells[dim]))
    return (
        masks[0][:, None, None] & masks[1][None, :, None] & masks[2][None, None, :]
    ).astype(jnp.float32)


def port_kernel(onehot_ref, spread_ref, coef_ref, tangent_ref, dft_ref, weight_ref, out_ref, part_ref):
    ports = dft_ref.shape[0]
    comps = spread_ref.shape[0]
    for p in range(ports):
        pick = onehot_ref[p:p + 1, :]
        acc = dft_ref[p]
        for step in range(coef_ref.shape[0]):
            inc = None
            for c in range(comps):
                plane = jnp.sum(tangent_ref[step * comps + c] * pick, axis=-1, keepdims=True)
                term = plane * spread_ref[c:c + 1, :]
                inc = term if inc is None else inc + term
            acc = acc + inc * coef_ref[step:step + 1, :]
        out_ref[p] = acc
        flat = acc.reshape(-1, acc.shape[-1])
        high = flat.astype(jnp.bfloat16)
        rest = flat - high.astype(jnp.float32)
        middle = rest.astype(jnp.bfloat16)
        low = (rest - middle.astype(jnp.float32)).astype(jnp.bfloat16)
        weight = weight_ref[p]
        total = jnp.dot(weight, high, preferred_element_type=jnp.float32)
        total = total + jnp.dot(weight, middle, preferred_element_type=jnp.float32)
        part_ref[p] = total + jnp.dot(weight, low, preferred_element_type=jnp.float32)


def per_device(e_field, h_field, inv_permittivity, dft_sums, omega, port_z, mode_profiles):
    cells = e_field.shape[1:]
    cells_x, cells_y, cells_z = cells
    ports_here = dft_sums.shape[0]
    stack = jnp.concatenate([e_field, h_field, inv_permittivity[None]], axis=0)
    stack = pin(widen(stack, 1, "gx"))
    stack = widen(stack, 2, "gy")
    spare = -stack.shape[2] % 8
    stack = pin(jnp.pad(stack, ((0, 0), (0, 0), (0, spare), (0, 0))))
    stack = pin(widen_lanes(stack, "gz"))
    e0, h0, inv = stack[0:3], stack[3:6], stack[6]
    n = lambda k: tuple(c + k for c in cells)
    h1 = box(h0, (0, 0, 0), n(3)) - 0.5 * curl(e0, (0, 0, 0), n(3), 1)
    h1 = pin(h1 * inside(-2, n(3), cells))
    e1 = pin(box(e0, (1, 1, 1), n(2)) + 0.5 * box(inv, (1, 1, 1), n(2)) * curl(h1, (1, 1, 1), n(2), -1))
    h2 = box(h1, (1, 1, 1), n(1)) - 0.5 * curl(e1, (0, 0, 0), n(1), 1)
    h2 = pin(h2 * inside(-1, n(1), cells))
    e2 = pin(box(e1, (1, 1, 1), n(0)) + 0.5 * box(inv, (2, 2, 2), n(0)) * curl(h2, (1, 1, 1), n(0), -1))
    e1_here = box(e1, (1, 1, 1), n(0))
    h1_here = box(h1, (2, 2, 2), n(0))
    h2_here = box(h2, (1, 1, 1), n(0))
    local_z = port_z - lax.axis_index("gz") * cells_z
    onehot = (local_z[:, None] == jnp.arange(cells_z)[None, :]).astype(jnp.float32)
    lanes = dft_sums.shape[-1]
    lane_part = jnp.arange(lanes) // (lanes // 4)
    spread_of = (lane_part[None, :] == jnp.arange(4)[:, None]).astype(jnp.float32)
    coefs = []
    for step in range(STEPS):
        phase = omega * jnp.float32(step + 1)
        coefs.append(jnp.tile(jnp.stack([jnp.cos(phase), jnp.sin(phase)]).reshape(-1), 4))
    coefs = jnp.stack(coefs)
    tangent = pin(jnp.concatenate([
        jnp.stack([e1_here[0], e1_here[1], h1_here[0], h1_here[1]]),
        jnp.stack([e2[0], e2[1], h2_here[0], h2_here[1]]),
    ]))
    groups = lax.axis_size(("gx", "gy"))
    owned = ports_here * NF // groups
    start_x = lax.axis_index("gx") * cells_x
    start_y = lax.axis_index("gy") * cells_y
    tile = lax.dynamic_slice(
        mode_profiles, (0, 0, 0, start_x, start_y), (ports_here, MODES, 4, cells_x, cells_y)
    )
    weights = tile.reshape(ports_here, MODES * 4, cells_x * cells_y)
    vmem = pl.BlockSpec(memory_space=pltpu.VMEM)
    dft, crossed = pl.pallas_call(
        port_kernel,
        out_shape=(
            jax.ShapeDtypeStruct(dft_sums.shape, jnp.float32),
            jax.ShapeDtypeStruct((ports_here, MODES * 4, lanes), jnp.float32),
        ),
        in_specs=[vmem] * 6,
        out_specs=(vmem, vmem),
    )(onehot, spread_of, coefs, tangent, dft_sums, weights)
    crossed = crossed.reshape(ports_here, MODES, 4, 4, 2, NF)
    diagonal = sum(crossed[:, :, c, c] for c in range(4))
    partial_sums = jnp.transpose(diagonal, (0, 3, 1, 2)).reshape(ports_here * NF, MODES * 2)
    pieces = partial_sums.reshape(groups, owned, MODES * 2)
    result = jnp.sum(lax.all_to_all(pieces, ("gx", "gy"), 0, 0, tiled=False), axis=0)
    return (e2, h2_here, dft, result.reshape(owned, 1, MODES * 2))


def solution(mesh):
    return jax.shard_map(
        per_device,
        mesh=mesh,
        in_specs=(
            P(None, "gx", "gy", "gz"),
            P(None, "gx", "gy", "gz"),
            P("gx", "gy", "gz"),
            P("gz", "gx", "gy", None),
            P(),
            P("gz"),
            P("gz", None, None, None, None),
        ),
        out_specs=(
            P(None, "gx", "gy", "gz"),
            P(None, "gx", "gy", "gz"),
            P("gz", "gx", "gy", None),
            P(("gx", "gy"), "gz", None),
        ),
        check_vma=False,
    )
```

```python
import jax
import jax.numpy as jnp
from jax import lax
from jax.sharding import PartitionSpec as P
from jax.experimental.layout import Layout, with_layout_constraint

STEPS = 2
NF = 16
MODES = 2
HALO = 2
AXES = ("gx", "gy", "gz")


def pin(value):
    return with_layout_constraint(value, Layout(tuple(range(value.ndim))))


def shifted(value, axis, steps):
    count = lax.axis_size(axis)
    first, last = (max(0, -steps), min(count, count - steps))
    return lax.ppermute(value, axis, [(source, source + steps) for source in range(first, last)])


def widen(stack, dim, axis):
    count = stack.shape[dim]
    low = lax.slice_in_dim(stack, 0, HALO, axis=dim)
    high = lax.slice_in_dim(stack, count - HALO, count, axis=dim)
    from_below = shifted(high, axis, 1)
    from_above = shifted(low, axis, -1)
    return jnp.concatenate([from_below, stack, from_above], axis=dim)


def widen_lanes(stack, axis):
    lanes = stack.shape[-1]
    flat = stack.reshape(-1, lanes)
    lane = jnp.arange(lanes)
    edges = jnp.concatenate([jnp.arange(HALO), jnp.arange(lanes - HALO, lanes)])
    pick = (lane[None, :] == edges[:, None]).astype(jnp.float32)
    faces = jnp.einsum("kz,rz->kr", pick, flat, precision=lax.Precision.HIGHEST)
    from_above = shifted(faces[:HALO], axis, -1)
    from_below = shifted(faces[HALO:], axis, 1)
    ghosts = jnp.concatenate([from_below, from_above], axis=0)
    out = jnp.arange(lanes + 2 * HALO)
    spots = jnp.concatenate([jnp.arange(HALO), jnp.arange(lanes + HALO, lanes + 2 * HALO)])
    move = (out[None, :] == lane[:, None] + HALO).astype(jnp.float32)
    place = (out[None, :] == spots[:, None]).astype(jnp.float32)
    wide = jnp.dot(flat, move, precision=lax.Precision.HIGHEST) + jnp.einsum(
        "kr,kl->rl", ghosts, place, precision=lax.Precision.HIGHEST
    )
    return wide.reshape(stack.shape[:-1] + (lanes + 2 * HALO,))


def box(value, start, size):
    lead = value.ndim - 3
    return lax.slice(
        value,
        (0,) * lead + tuple(start),
        value.shape[:lead] + tuple(s + n for s, n in zip(start, size)),
    )


def moved(start, dim, step):
    return tuple(s + step if d == dim else s for d, s in enumerate(start))


def differ(value, start, size, dim, step):
    if step > 0:
        return box(value, moved(start, dim, 1), size) - box(value, start, size)
    return box(value, start, size) - box(value, moved(start, dim, -1), size)


def curl(field, start, size, step):
    vx, vy, vz = field[0], field[1], field[2]
    d = lambda v, dim: differ(v, start, size, dim, step)
    return jnp.stack([d(vz, 1) - d(vy, 2), d(vx, 2) - d(vz, 0), d(vy, 0) - d(vx, 1)])


def inside(origin, size, cells):
    keep = None
    for dim, axis in enumerate(AXES):
        first = lax.axis_index(axis) * cells[dim] + origin
        where = lax.broadcasted_iota(jnp.int32, size, dim) + first
        test = (where >= 0) & (where < lax.axis_size(axis) * cells[dim])
        keep = test if keep is None else keep & test
    return keep


def per_device(e_field, h_field, inv_permittivity, dft_sums, omega, port_z, mode_profiles):
    cells = e_field.shape[1:]
    cells_x, cells_y, cells_z = cells
    ports_here = dft_sums.shape[0]
    stack = jnp.concatenate([e_field, h_field, inv_permittivity[None]], axis=0)
    stack = pin(widen(stack, 1, "gx"))
    stack = widen(stack, 2, "gy")
    spare = -stack.shape[2] % 8
    stack = pin(jnp.pad(stack, ((0, 0), (0, 0), (0, spare), (0, 0))))
    stack = pin(widen_lanes(stack, "gz"))
    e0, h0, inv = stack[0:3], stack[3:6], stack[6]
    n = lambda k: tuple(c + k for c in cells)
    h1 = box(h0, (0, 0, 0), n(3)) - 0.5 * curl(e0, (0, 0, 0), n(3), 1)
    h1 = pin(jnp.where(inside(-2, n(3), cells), h1, 0.0))
    e1 = pin(box(e0, (1, 1, 1), n(2)) + 0.5 * box(inv, (1, 1, 1), n(2)) * curl(h1, (1, 1, 1), n(2), -1))
    h2 = box(h1, (1, 1, 1), n(1)) - 0.5 * curl(e1, (0, 0, 0), n(1), 1)
    h2 = pin(jnp.where(inside(-1, n(1), cells), h2, 0.0))
    e2 = pin(box(e1, (1, 1, 1), n(0)) + 0.5 * box(inv, (2, 2, 2), n(0)) * curl(h2, (1, 1, 1), n(0), -1))
    e1_here = box(e1, (1, 1, 1), n(0))
    h1_here = box(h1, (2, 2, 2), n(0))
    h2_here = box(h2, (1, 1, 1), n(0))
    local_z = port_z - lax.axis_index("gz") * cells_z
    onehot = (local_z[:, None] == jnp.arange(cells_z)[None, :]).astype(jnp.float32)
    lanes = dft_sums.shape[-1]
    lane_part = jnp.arange(lanes) // (lanes // 4)
    spread_of = (lane_part[None, :] == jnp.arange(4)[:, None]).astype(jnp.float32)
    dft = dft_sums
    for step, (e_now, h_now) in enumerate(((e1_here, h1_here), (e2, h2_here))):
        tangent = pin(jnp.stack([e_now[0], e_now[1], h_now[0], h_now[1]]))
        planes = jnp.sum(tangent[None] * onehot[:, None, None, None, :], axis=-1)
        phase = omega * jnp.float32(step + 1)
        trig = jnp.stack([jnp.cos(phase), jnp.sin(phase)])
        coef = jnp.tile(trig.reshape(-1), 4)
        spread = jnp.sum(planes[..., None] * spread_of[None, :, None, None, :], axis=1)
        dft = pin(dft + spread * coef)
    groups = lax.axis_size(("gx", "gy"))
    owned = ports_here * NF // groups
    start_x = lax.axis_index("gx") * cells_x
    start_y = lax.axis_index("gy") * cells_y
    tile = lax.dynamic_slice(
        mode_profiles, (0, 0, 0, start_x, start_y), (ports_here, MODES, 4, cells_x, cells_y)
    )
    weights = tile.reshape(ports_here, MODES * 4, cells_x, cells_y).astype(jnp.float32)
    crossed = jnp.einsum("pxyl,pnxy->pnl", dft, weights, precision=lax.Precision.HIGHEST)
    crossed = crossed.reshape(ports_here, MODES, 4, 4, 2, NF)
    diagonal = sum(crossed[:, :, c, c] for c in range(4))
    partial_sums = jnp.transpose(diagonal, (0, 3, 1, 2)).reshape(ports_here * NF, MODES * 2)
    pieces = partial_sums.reshape(groups, owned, MODES * 2)
    result = jnp.sum(lax.all_to_all(pieces, ("gx", "gy"), 0, 0, tiled=False), axis=0)
    return (e2, h2_here, dft, result.reshape(owned, 1, MODES * 2))


def solution(mesh):
    return jax.shard_map(
        per_device,
        mesh=mesh,
        in_specs=(
            P(None, "gx", "gy", "gz"),
            P(None, "gx", "gy", "gz"),
            P("gx", "gy", "gz"),
            P("gz", "gx", "gy", None),
            P(),
            P("gz"),
            P("gz", None, None, None, None),
        ),
        out_specs=(
            P(None, "gx", "gy", "gz"),
            P(None, "gx", "gy", "gz"),
            P("gz", "gx", "gy", None),
            P(("gx", "gy"), "gz", None),
        ),
        check_vma=False,
    )
```

```python
import jax
import jax.numpy as jnp
from jax import lax
from jax.sharding import PartitionSpec as P
from jax.experimental.layout import Layout, with_layout_constraint

STEPS = 2
NF = 16
MODES = 2
HALO = 2
AXES = ("gx", "gy", "gz")


def pin(value):
    return with_layout_constraint(value, Layout(tuple(range(value.ndim))))


def shifted(value, axis, steps):
    count = lax.axis_size(axis)
    first, last = (max(0, -steps), min(count, count - steps))
    return lax.ppermute(value, axis, [(source, source + steps) for source in range(first, last)])


def widen(stack, dim, axis):
    count = stack.shape[dim]
    low = lax.slice_in_dim(stack, 0, HALO, axis=dim)
    high = lax.slice_in_dim(stack, count - HALO, count, axis=dim)
    from_below = shifted(high, axis, 1)
    from_above = shifted(low, axis, -1)
    return jnp.concatenate([from_below, stack, from_above], axis=dim)


def widen_lanes(stack, axis):
    lanes = stack.shape[-1]
    flat = stack.reshape(-1, lanes)
    lane = jnp.arange(lanes)
    edges = jnp.concatenate([jnp.arange(HALO), jnp.arange(lanes - HALO, lanes)])
    pick = (lane[None, :] == edges[:, None]).astype(jnp.float32)
    faces = jnp.einsum("kz,rz->kr", pick, flat, precision=lax.Precision.HIGHEST)
    from_above = shifted(faces[:HALO], axis, -1)
    from_below = shifted(faces[HALO:], axis, 1)
    ghosts = jnp.concatenate([from_below, from_above], axis=0)
    out = jnp.arange(lanes + 2 * HALO)
    spots = jnp.concatenate([jnp.arange(HALO), jnp.arange(lanes + HALO, lanes + 2 * HALO)])
    move = (out[None, :] == lane[:, None] + HALO).astype(jnp.float32)
    place = (out[None, :] == spots[:, None]).astype(jnp.float32)
    wide = jnp.dot(flat, move, precision=lax.Precision.HIGHEST) + jnp.einsum(
        "kr,kl->rl", ghosts, place, precision=lax.Precision.HIGHEST
    )
    return wide.reshape(stack.shape[:-1] + (lanes + 2 * HALO,))


def box(value, start, size):
    lead = value.ndim - 3
    return lax.slice(
        value,
        (0,) * lead + tuple(start),
        value.shape[:lead] + tuple(s + n for s, n in zip(start, size)),
    )


def moved(start, dim, step):
    return tuple(s + step if d == dim else s for d, s in enumerate(start))


def differ(value, start, size, dim, step):
    if step > 0:
        return box(value, moved(start, dim, 1), size) - box(value, start, size)
    return box(value, start, size) - box(value, moved(start, dim, -1), size)


def curl(field, start, size, step):
    vx, vy, vz = field
    d = lambda v, dim: differ(v, start, size, dim, step)
    return [d(vz, 1) - d(vy, 2), d(vx, 2) - d(vz, 0), d(vy, 0) - d(vx, 1)]


def inside(origin, size, cells):
    masks = []
    for dim, axis in enumerate(AXES):
        count = lax.axis_size(axis)
        first = lax.axis_index(axis) * cells[dim] + origin
        where = first + jnp.arange(size[dim])
        masks.append((where >= 0) & (where < count * cells[dim]))
    return (
        masks[0][:, None, None] & masks[1][None, :, None] & masks[2][None, None, :]
    ).astype(jnp.float32)


def per_device(e_field, h_field, inv_permittivity, dft_sums, omega, port_z, mode_profiles):
    cells = e_field.shape[1:]
    cells_x, cells_y, cells_z = cells
    ports_here = dft_sums.shape[0]
    stack = jnp.concatenate([e_field, h_field, inv_permittivity[None]], axis=0)
    stack = pin(widen(stack, 1, "gx"))
    stack = widen(stack, 2, "gy")
    spare = -stack.shape[2] % 8
    stack = pin(jnp.pad(stack, ((0, 0), (0, 0), (0, spare), (0, 0))))
    stack = pin(widen_lanes(stack, "gz"))
    e0 = [stack[i] for i in range(3)]
    h0 = [stack[3 + i] for i in range(3)]
    inv = stack[6]
    n = lambda k: tuple(c + k for c in cells)
    at = lambda v, k, size: box(v, (k, k, k), size)
    keep = inside(-2, n(3), cells)
    h1 = [pin((at(v, 0, n(3)) - 0.5 * c) * keep) for v, c in zip(h0, curl(e0, (0, 0, 0), n(3), 1))]
    scale = 0.5 * at(inv, 1, n(2))
    e1 = [pin(at(v, 1, n(2)) + scale * c) for v, c in zip(e0, curl(h1, (1, 1, 1), n(2), -1))]
    keep = inside(-1, n(1), cells)
    h2 = [pin((at(v, 1, n(1)) - 0.5 * c) * keep) for v, c in zip(h1, curl(e1, (0, 0, 0), n(1), 1))]
    scale = 0.5 * at(inv, 2, n(0))
    e2 = [at(v, 1, n(0)) + scale * c for v, c in zip(e1, curl(h2, (1, 1, 1), n(0), -1))]
    e1_here = [at(v, 1, n(0)) for v in e1]
    h1_here = [at(v, 2, n(0)) for v in h1]
    h2_here = [at(v, 1, n(0)) for v in h2]
    local_z = port_z - lax.axis_index("gz") * cells_z
    onehot = (local_z[:, None] == jnp.arange(cells_z)[None, :]).astype(jnp.float32)
    lanes = dft_sums.shape[-1]
    lane_part = jnp.arange(lanes) // (lanes // 4)
    spread_of = (lane_part[None, :] == jnp.arange(4)[:, None]).astype(jnp.float32)
    dft = dft_sums
    for step, (e_now, h_now) in enumerate(((e1_here, h1_here), (e2, h2_here))):
        tangent = pin(jnp.stack([e_now[0], e_now[1], h_now[0], h_now[1]]))
        planes = jnp.sum(tangent[None] * onehot[:, None, None, None, :], axis=-1)
        phase = omega * jnp.float32(step + 1)
        trig = jnp.stack([jnp.cos(phase), jnp.sin(phase)])
        coef = jnp.tile(trig.reshape(-1), 4)
        spread = jnp.sum(planes[..., None] * spread_of[None, :, None, None, :], axis=1)
        dft = pin(dft + spread * coef)
    groups = lax.axis_size(("gx", "gy"))
    owned = ports_here * NF // groups
    start_x = lax.axis_index("gx") * cells_x
    start_y = lax.axis_index("gy") * cells_y
    tile = lax.dynamic_slice(
        mode_profiles, (0, 0, 0, start_x, start_y), (ports_here, MODES, 4, cells_x, cells_y)
    )
    weights = tile.reshape(ports_here, MODES * 4, cells_x, cells_y).astype(jnp.float32)
    crossed = jnp.einsum("pxyl,pnxy->pnl", dft, weights, precision=lax.Precision.HIGHEST)
    crossed = crossed.reshape(ports_here, MODES, 4, 4, 2, NF)
    diagonal = sum(crossed[:, :, c, c] for c in range(4))
    partial_sums = jnp.transpose(diagonal, (0, 3, 1, 2)).reshape(ports_here * NF, MODES * 2)
    pieces = partial_sums.reshape(groups, owned, MODES * 2)
    result = jnp.sum(lax.all_to_all(pieces, ("gx", "gy"), 0, 0, tiled=False), axis=0)
    return (jnp.stack(e2), jnp.stack(h2_here), dft, result.reshape(owned, 1, MODES * 2))


def solution(mesh):
    return jax.shard_map(
        per_device,
        mesh=mesh,
        in_specs=(
            P(None, "gx", "gy", "gz"),
            P(None, "gx", "gy", "gz"),
            P("gx", "gy", "gz"),
            P("gz", "gx", "gy", None),
            P(),
            P("gz"),
            P("gz", None, None, None, None),
        ),
        out_specs=(
            P(None, "gx", "gy", "gz"),
            P(None, "gx", "gy", "gz"),
            P("gz", "gx", "gy", None),
            P(("gx", "gy"), "gz", None),
        ),
        check_vma=False,
    )
```

```python
import jax
import jax.numpy as jnp
from jax import lax
from jax.sharding import PartitionSpec as P
from jax.experimental.layout import Layout, with_layout_constraint

STEPS = 2
NF = 16
MODES = 2
HALO = 2
AXES = ("gx", "gy", "gz")


def pin(value):
    return with_layout_constraint(value, Layout(tuple(range(value.ndim))))


def shifted(value, axis, steps):
    count = lax.axis_size(axis)
    first, last = (max(0, -steps), min(count, count - steps))
    return lax.ppermute(value, axis, [(source, source + steps) for source in range(first, last)])


def widen(stack, dim, axis):
    count = stack.shape[dim]
    low = lax.slice_in_dim(stack, 0, HALO, axis=dim)
    high = lax.slice_in_dim(stack, count - HALO, count, axis=dim)
    from_below = shifted(high, axis, 1)
    from_above = shifted(low, axis, -1)
    return jnp.concatenate([from_below, stack, from_above], axis=dim)


def widen_lanes(stack, axis):
    lanes = stack.shape[-1]
    flat = stack.reshape(-1, lanes)
    lane = jnp.arange(lanes)
    edges = jnp.concatenate([jnp.arange(HALO), jnp.arange(lanes - HALO, lanes)])
    pick = (lane[None, :] == edges[:, None]).astype(jnp.float32)
    faces = jnp.einsum("kz,rz->kr", pick, flat, precision=lax.Precision.HIGHEST)
    from_above = shifted(faces[:HALO], axis, -1)
    from_below = shifted(faces[HALO:], axis, 1)
    ghosts = jnp.concatenate([from_below, from_above], axis=0)
    out = jnp.arange(lanes + 2 * HALO)
    spots = jnp.concatenate([jnp.arange(HALO), jnp.arange(lanes + HALO, lanes + 2 * HALO)])
    move = (out[None, :] == lane[:, None] + HALO).astype(jnp.float32)
    place = (out[None, :] == spots[:, None]).astype(jnp.float32)
    wide = jnp.dot(flat, move, precision=lax.Precision.HIGHEST) + jnp.einsum(
        "kr,kl->rl", ghosts, place, precision=lax.Precision.HIGHEST
    )
    return wide.reshape(stack.shape[:-1] + (lanes + 2 * HALO,))


def box(value, start, size):
    lead = value.ndim - 3
    return lax.slice(
        value,
        (0,) * lead + tuple(start),
        value.shape[:lead] + tuple(s + n for s, n in zip(start, size)),
    )


def moved(start, dim, step):
    return tuple(s + step if d == dim else s for d, s in enumerate(start))


def differ(value, start, size, dim, step):
    if step > 0:
        return box(value, moved(start, dim, 1), size) - box(value, start, size)
    return box(value, start, size) - box(value, moved(start, dim, -1), size)


def curl(field, start, size, step):
    vx, vy, vz = field
    d = lambda v, dim: differ(v, start, size, dim, step)
    return [d(vz, 1) - d(vy, 2), d(vx, 2) - d(vz, 0), d(vy, 0) - d(vx, 1)]


def inside(origin, size, cells):
    masks = []
    for dim, axis in enumerate(AXES):
        count = lax.axis_size(axis)
        first = lax.axis_index(axis) * cells[dim] + origin
        where = first + jnp.arange(size[dim])
        masks.append((where >= 0) & (where < count * cells[dim]))
    return (
        masks[0][:, None, None] & masks[1][None, :, None] & masks[2][None, None, :]
    ).astype(jnp.float32)


def per_device(e_field, h_field, inv_permittivity, dft_sums, omega, port_z, mode_profiles):
    cells = e_field.shape[1:]
    cells_x, cells_y, cells_z = cells
    ports_here = dft_sums.shape[0]
    stack = jnp.concatenate([e_field, h_field, inv_permittivity[None]], axis=0)
    stack = pin(widen(stack, 1, "gx"))
    stack = widen(stack, 2, "gy")
    spare = -stack.shape[2] % 8
    stack = pin(jnp.pad(stack, ((0, 0), (0, 0), (0, spare), (0, 0))))
    stack = pin(widen_lanes(stack, "gz"))
    e0 = [stack[i] for i in range(3)]
    h0 = [stack[3 + i] for i in range(3)]
    inv = stack[6]
    n = lambda k: tuple(c + k for c in cells)
    at = lambda v, k, size: box(v, (k, k, k), size)
    keep = inside(-2, n(3), cells)
    h1 = [pin((at(v, 0, n(3)) - 0.5 * c) * keep) for v, c in zip(h0, curl(e0, (0, 0, 0), n(3), 1))]
    scale = 0.5 * at(inv, 1, n(2))
    e1 = [pin(at(v, 1, n(2)) + scale * c) for v, c in zip(e0, curl(h1, (1, 1, 1), n(2), -1))]
    keep = inside(-1, n(1), cells)
    h2 = [pin((at(v, 1, n(1)) - 0.5 * c) * keep) for v, c in zip(h1, curl(e1, (0, 0, 0), n(1), 1))]
    scale = 0.5 * at(inv, 2, n(0))
    e2 = [at(v, 1, n(0)) + scale * c for v, c in zip(e1, curl(h2, (1, 1, 1), n(0), -1))]
    e1_here = [at(v, 1, n(0)) for v in e1]
    h1_here = [at(v, 2, n(0)) for v in h1]
    h2_here = [at(v, 1, n(0)) for v in h2]
    local_z = port_z - lax.axis_index("gz") * cells_z
    onehot = (local_z[:, None] == jnp.arange(cells_z)[None, :]).astype(jnp.float32)
    lanes = dft_sums.shape[-1]
    lane_part = jnp.arange(lanes) // (lanes // 4)
    spread_of = (lane_part[None, :] == jnp.arange(4)[:, None]).astype(jnp.float32)
    dft = dft_sums
    both = ((e1_here, h1_here), (e2, h2_here))
    tangent = pin(jnp.stack([v for e_now, h_now in both for v in (e_now[0], e_now[1], h_now[0], h_now[1])]))
    every_plane = jnp.sum(tangent[None] * onehot[:, None, None, None, :], axis=-1)
    for step in range(STEPS):
        planes = every_plane[:, 4 * step:4 * step + 4]
        phase = omega * jnp.float32(step + 1)
        trig = jnp.stack([jnp.cos(phase), jnp.sin(phase)])
        coef = jnp.tile(trig.reshape(-1), 4)
        spread = jnp.sum(planes[..., None] * spread_of[None, :, None, None, :], axis=1)
        dft = pin(dft + spread * coef)
    groups = lax.axis_size(("gx", "gy"))
    owned = ports_here * NF // groups
    start_x = lax.axis_index("gx") * cells_x
    start_y = lax.axis_index("gy") * cells_y
    tile = lax.dynamic_slice(
        mode_profiles, (0, 0, 0, start_x, start_y), (ports_here, MODES, 4, cells_x, cells_y)
    )
    weights = tile.reshape(ports_here, MODES * 4, cells_x, cells_y).astype(jnp.float32)
    crossed = jnp.einsum("pxyl,pnxy->pnl", dft, weights, precision=lax.Precision.HIGHEST)
    crossed = crossed.reshape(ports_here, MODES, 4, 4, 2, NF)
    diagonal = sum(crossed[:, :, c, c] for c in range(4))
    partial_sums = jnp.transpose(diagonal, (0, 3, 1, 2)).reshape(ports_here * NF, MODES * 2)
    pieces = partial_sums.reshape(groups, owned, MODES * 2)
    result = jnp.sum(lax.all_to_all(pieces, ("gx", "gy"), 0, 0, tiled=False), axis=0)
    return (jnp.stack(e2), jnp.stack(h2_here), dft, result.reshape(owned, 1, MODES * 2))


def solution(mesh):
    return jax.shard_map(
        per_device,
        mesh=mesh,
        in_specs=(
            P(None, "gx", "gy", "gz"),
            P(None, "gx", "gy", "gz"),
            P("gx", "gy", "gz"),
            P("gz", "gx", "gy", None),
            P(),
            P("gz"),
            P("gz", None, None, None, None),
        ),
        out_specs=(
            P(None, "gx", "gy", "gz"),
            P(None, "gx", "gy", "gz"),
            P("gz", "gx", "gy", None),
            P(("gx", "gy"), "gz", None),
        ),
        check_vma=False,
    )
```

```python
import jax
import jax.numpy as jnp
from jax import lax
from jax.sharding import PartitionSpec as P
from jax.experimental.layout import Layout, with_layout_constraint

STEPS = 2
NF = 16
MODES = 2
HALO = 2
AXES = ("gx", "gy", "gz")


def pin(value):
    return with_layout_constraint(value, Layout(tuple(range(value.ndim))))


def shifted(value, axis, steps):
    count = lax.axis_size(axis)
    first, last = (max(0, -steps), min(count, count - steps))
    return lax.ppermute(value, axis, [(source, source + steps) for source in range(first, last)])


def widen(stack, dim, axis):
    count = stack.shape[dim]
    low = lax.slice_in_dim(stack, 0, HALO, axis=dim)
    high = lax.slice_in_dim(stack, count - HALO, count, axis=dim)
    from_below = shifted(high, axis, 1)
    from_above = shifted(low, axis, -1)
    return jnp.concatenate([from_below, stack, from_above], axis=dim)


def widen_lanes(stack, axis):
    lanes = stack.shape[-1]
    flat = stack.reshape(-1, lanes)
    lane = jnp.arange(lanes)
    edges = jnp.concatenate([jnp.arange(HALO), jnp.arange(lanes - HALO, lanes)])
    pick = (lane[None, :] == edges[:, None]).astype(jnp.float32)
    faces = jnp.einsum("kz,rz->kr", pick, flat, precision=lax.Precision.HIGHEST)
    from_above = shifted(faces[:HALO], axis, -1)
    from_below = shifted(faces[HALO:], axis, 1)
    ghosts = jnp.concatenate([from_below, from_above], axis=0)
    out = jnp.arange(lanes + 2 * HALO)
    spots = jnp.concatenate([jnp.arange(HALO), jnp.arange(lanes + HALO, lanes + 2 * HALO)])
    move = (out[None, :] == lane[:, None] + HALO).astype(jnp.float32)
    place = (out[None, :] == spots[:, None]).astype(jnp.float32)
    wide = jnp.dot(flat, move, precision=lax.Precision.HIGHEST) + jnp.einsum(
        "kr,kl->rl", ghosts, place, precision=lax.Precision.HIGHEST
    )
    return wide.reshape(stack.shape[:-1] + (lanes + 2 * HALO,))


def box(value, start, size):
    lead = value.ndim - 3
    return lax.slice(
        value,
        (0,) * lead + tuple(start),
        value.shape[:lead] + tuple(s + n for s, n in zip(start, size)),
    )


def moved(start, dim, step):
    return tuple(s + step if d == dim else s for d, s in enumerate(start))


def differ(value, start, size, dim, step):
    if step > 0:
        return box(value, moved(start, dim, 1), size) - box(value, start, size)
    return box(value, start, size) - box(value, moved(start, dim, -1), size)


def curl(field, start, size, step):
    vx, vy, vz = field
    d = lambda v, dim: differ(v, start, size, dim, step)
    return [d(vz, 1) - d(vy, 2), d(vx, 2) - d(vz, 0), d(vy, 0) - d(vx, 1)]


def inside(origin, size, cells):
    masks = []
    for dim, axis in enumerate(AXES):
        count = lax.axis_size(axis)
        first = lax.axis_index(axis) * cells[dim] + origin
        where = first + jnp.arange(size[dim])
        masks.append((where >= 0) & (where < count * cells[dim]))
    return (
        masks[0][:, None, None] & masks[1][None, :, None] & masks[2][None, None, :]
    ).astype(jnp.float32)


def per_device(e_field, h_field, inv_permittivity, dft_sums, omega, port_z, mode_profiles):
    cells = e_field.shape[1:]
    cells_x, cells_y, cells_z = cells
    ports_here = dft_sums.shape[0]
    stack = jnp.concatenate([e_field, h_field, inv_permittivity[None]], axis=0)
    stack = pin(widen(stack, 2, "gy"))
    stack = widen(stack, 1, "gx")
    spare = -stack.shape[2] % 8
    stack = pin(jnp.pad(stack, ((0, 0), (0, 0), (0, spare), (0, 0))))
    stack = pin(widen_lanes(stack, "gz"))
    e0 = [stack[i] for i in range(3)]
    h0 = [stack[3 + i] for i in range(3)]
    inv = stack[6]
    n = lambda k: tuple(c + k for c in cells)
    at = lambda v, k, size: box(v, (k, k, k), size)
    keep = inside(-2, n(3), cells)
    h1 = [pin((at(v, 0, n(3)) - 0.5 * c) * keep) for v, c in zip(h0, curl(e0, (0, 0, 0), n(3), 1))]
    scale = 0.5 * at(inv, 1, n(2))
    e1 = [pin(at(v, 1, n(2)) + scale * c) for v, c in zip(e0, curl(h1, (1, 1, 1), n(2), -1))]
    keep = inside(-1, n(1), cells)
    h2 = [pin((at(v, 1, n(1)) - 0.5 * c) * keep) for v, c in zip(h1, curl(e1, (0, 0, 0), n(1), 1))]
    scale = 0.5 * at(inv, 2, n(0))
    e2 = [at(v, 1, n(0)) + scale * c for v, c in zip(e1, curl(h2, (1, 1, 1), n(0), -1))]
    e1_here = [at(v, 1, n(0)) for v in e1]
    h1_here = [at(v, 2, n(0)) for v in h1]
    h2_here = [at(v, 1, n(0)) for v in h2]
    local_z = port_z - lax.axis_index("gz") * cells_z
    onehot = (local_z[:, None] == jnp.arange(cells_z)[None, :]).astype(jnp.float32)
    lanes = dft_sums.shape[-1]
    lane_part = jnp.arange(lanes) // (lanes // 4)
    spread_of = (lane_part[None, :] == jnp.arange(4)[:, None]).astype(jnp.float32)
    dft = dft_sums
    for step, (e_now, h_now) in enumerate(((e1_here, h1_here), (e2, h2_here))):
        tangent = pin(jnp.stack([e_now[0], e_now[1], h_now[0], h_now[1]]))
        planes = jnp.sum(tangent[None] * onehot[:, None, None, None, :], axis=-1)
        phase = omega * jnp.float32(step + 1)
        trig = jnp.stack([jnp.cos(phase), jnp.sin(phase)])
        coef = jnp.tile(trig.reshape(-1), 4)
        spread = jnp.sum(planes[..., None] * spread_of[None, :, None, None, :], axis=1)
        dft = pin(dft + spread * coef)
    groups = lax.axis_size(("gx", "gy"))
    owned = ports_here * NF // groups
    start_x = lax.axis_index("gx") * cells_x
    start_y = lax.axis_index("gy") * cells_y
    tile = lax.dynamic_slice(
        mode_profiles, (0, 0, 0, start_x, start_y), (ports_here, MODES, 4, cells_x, cells_y)
    )
    weights = tile.reshape(ports_here, MODES * 4, cells_x, cells_y).astype(jnp.float32)
    crossed = jnp.einsum("pxyl,pnxy->pnl", dft, weights, precision=lax.Precision.HIGHEST)
    crossed = crossed.reshape(ports_here, MODES, 4, 4, 2, NF)
    diagonal = sum(crossed[:, :, c, c] for c in range(4))
    partial_sums = jnp.transpose(diagonal, (0, 3, 1, 2)).reshape(ports_here * NF, MODES * 2)
    pieces = partial_sums.reshape(groups, owned, MODES * 2)
    result = jnp.sum(lax.all_to_all(pieces, ("gx", "gy"), 0, 0, tiled=False), axis=0)
    return (jnp.stack(e2), jnp.stack(h2_here), dft, result.reshape(owned, 1, MODES * 2))


def solution(mesh):
    return jax.shard_map(
        per_device,
        mesh=mesh,
        in_specs=(
            P(None, "gx", "gy", "gz"),
            P(None, "gx", "gy", "gz"),
            P("gx", "gy", "gz"),
            P("gz", "gx", "gy", None),
            P(),
            P("gz"),
            P("gz", None, None, None, None),
        ),
        out_specs=(
            P(None, "gx", "gy", "gz"),
            P(None, "gx", "gy", "gz"),
            P("gz", "gx", "gy", None),
            P(("gx", "gy"), "gz", None),
        ),
        check_vma=False,
    )
```

```python
import jax
import jax.numpy as jnp
from jax import lax
from jax.sharding import PartitionSpec as P
from jax.experimental.layout import Layout, with_layout_constraint

STEPS = 2
NF = 16
MODES = 2
HALO = 2
AXES = ("gx", "gy", "gz")


def pin(value):
    return with_layout_constraint(value, Layout(tuple(range(value.ndim))))


def shifted(value, axis, steps):
    count = lax.axis_size(axis)
    first, last = (max(0, -steps), min(count, count - steps))
    return lax.ppermute(value, axis, [(source, source + steps) for source in range(first, last)])


def widen(stack, dim, axis):
    count = stack.shape[dim]
    low = lax.slice_in_dim(stack, 0, HALO, axis=dim)
    high = lax.slice_in_dim(stack, count - HALO, count, axis=dim)
    from_below = shifted(high, axis, 1)
    from_above = shifted(low, axis, -1)
    return jnp.concatenate([from_below, stack, from_above], axis=dim)


def widen_lanes(stack, axis):
    lanes = stack.shape[-1]
    flat = stack.reshape(-1, lanes)
    lane = jnp.arange(lanes)
    edges = jnp.concatenate([jnp.arange(HALO), jnp.arange(lanes - HALO, lanes)])
    pick = (lane[None, :] == edges[:, None]).astype(jnp.float32)
    faces = jnp.einsum("kz,rz->kr", pick, flat, precision=lax.Precision.HIGHEST)
    from_above = shifted(faces[:HALO], axis, -1)
    from_below = shifted(faces[HALO:], axis, 1)
    ghosts = jnp.concatenate([from_below, from_above], axis=0)
    out = jnp.arange(lanes + 2 * HALO)
    spots = jnp.concatenate([jnp.arange(HALO), jnp.arange(lanes + HALO, lanes + 2 * HALO)])
    move = (out[None, :] == lane[:, None] + HALO).astype(jnp.float32)
    place = (out[None, :] == spots[:, None]).astype(jnp.float32)
    wide = jnp.dot(flat, move, precision=lax.Precision.HIGHEST) + jnp.einsum(
        "kr,kl->rl", ghosts, place, precision=lax.Precision.HIGHEST
    )
    return wide.reshape(stack.shape[:-1] + (lanes + 2 * HALO,))


def box(value, start, size):
    lead = value.ndim - 3
    return lax.slice(
        value,
        (0,) * lead + tuple(start),
        value.shape[:lead] + tuple(s + n for s, n in zip(start, size)),
    )


def moved(start, dim, step):
    return tuple(s + step if d == dim else s for d, s in enumerate(start))


def differ(value, start, size, dim, step):
    if step > 0:
        return box(value, moved(start, dim, 1), size) - box(value, start, size)
    return box(value, start, size) - box(value, moved(start, dim, -1), size)


def curl(field, start, size, step):
    vx, vy, vz = field
    d = lambda v, dim: differ(v, start, size, dim, step)
    return [d(vz, 1) - d(vy, 2), d(vx, 2) - d(vz, 0), d(vy, 0) - d(vx, 1)]


def inside(origin, size, cells):
    masks = []
    for dim, axis in enumerate(AXES):
        count = lax.axis_size(axis)
        first = lax.axis_index(axis) * cells[dim] + origin
        where = first + jnp.arange(size[dim])
        masks.append((where >= 0) & (where < count * cells[dim]))
    return (
        masks[0][:, None, None] & masks[1][None, :, None] & masks[2][None, None, :]
    ).astype(jnp.float32)


def per_device(e_field, h_field, inv_permittivity, dft_sums, omega, port_z, mode_profiles):
    cells = e_field.shape[1:]
    cells_x, cells_y, cells_z = cells
    ports_here = dft_sums.shape[0]
    stack = jnp.concatenate([e_field, h_field, inv_permittivity[None]], axis=0)
    stack = pin(widen(stack, 2, "gy"))
    stack = widen(stack, 1, "gx")
    spare = -stack.shape[2] % 8
    stack = pin(jnp.pad(stack, ((0, 0), (0, 0), (0, spare), (0, 0))))
    stack = pin(widen_lanes(stack, "gz"))
    e0 = [stack[i] for i in range(3)]
    h0 = [stack[3 + i] for i in range(3)]
    inv = stack[6]
    n = lambda k: tuple(c + k for c in cells)
    at = lambda v, k, size: box(v, (k, k, k), size)
    keep = inside(-2, n(3), cells)
    h1 = [pin((at(v, 0, n(3)) - 0.5 * c) * keep) for v, c in zip(h0, curl(e0, (0, 0, 0), n(3), 1))]
    scale = 0.5 * at(inv, 1, n(2))
    e1 = [pin(at(v, 1, n(2)) + scale * c) for v, c in zip(e0, curl(h1, (1, 1, 1), n(2), -1))]
    keep = inside(-1, n(1), cells)
    h2 = [pin((at(v, 1, n(1)) - 0.5 * c) * keep) for v, c in zip(h1, curl(e1, (0, 0, 0), n(1), 1))]
    scale = 0.5 * at(inv, 2, n(0))
    e2 = [at(v, 1, n(0)) + scale * c for v, c in zip(e1, curl(h2, (1, 1, 1), n(0), -1))]
    e1_here = [at(v, 1, n(0)) for v in e1]
    h1_here = [at(v, 2, n(0)) for v in h1]
    h2_here = [at(v, 1, n(0)) for v in h2]
    local_z = port_z - lax.axis_index("gz") * cells_z
    onehot = (local_z[:, None] == jnp.arange(cells_z)[None, :]).astype(jnp.float32)
    lanes = dft_sums.shape[-1]
    lane_part = jnp.arange(lanes) // (lanes // 4)
    spread_of = (lane_part[None, :] == jnp.arange(4)[:, None]).astype(jnp.float32)
    dft = dft_sums
    for step, (e_now, h_now) in enumerate(((e1_here, h1_here), (e2, h2_here))):
        tangent = pin(jnp.stack([e_now[0], e_now[1], h_now[0], h_now[1]]))
        planes = jnp.sum(tangent[None] * onehot[:, None, None, None, :], axis=-1)
        phase = omega * jnp.float32(step + 1)
        trig = jnp.stack([jnp.cos(phase), jnp.sin(phase)])
        coef = jnp.tile(trig.reshape(-1), 4)
        spread = jnp.sum(planes[..., None] * spread_of[None, :, None, None, :], axis=1)
        dft = pin(dft + spread * coef)
    groups = lax.axis_size(("gx", "gy"))
    owned = ports_here * NF // groups
    start_x = lax.axis_index("gx") * cells_x
    start_y = lax.axis_index("gy") * cells_y
    tile = lax.dynamic_slice(
        mode_profiles, (0, 0, 0, start_x, start_y), (ports_here, MODES, 4, cells_x, cells_y)
    )
    weights = tile.reshape(ports_here, MODES * 4, cells_x, cells_y).astype(jnp.float32)
    crossed = jnp.einsum("pxyl,pnxy->pnl", dft, weights, precision=lax.Precision.HIGH)
    crossed = crossed.reshape(ports_here, MODES, 4, 4, 2, NF)
    diagonal = sum(crossed[:, :, c, c] for c in range(4))
    partial_sums = jnp.transpose(diagonal, (0, 3, 1, 2)).reshape(ports_here * NF, MODES * 2)
    pieces = partial_sums.reshape(groups, owned, MODES * 2)
    result = jnp.sum(lax.all_to_all(pieces, ("gx", "gy"), 0, 0, tiled=False), axis=0)
    return (jnp.stack(e2), jnp.stack(h2_here), dft, result.reshape(owned, 1, MODES * 2))


def solution(mesh):
    return jax.shard_map(
        per_device,
        mesh=mesh,
        in_specs=(
            P(None, "gx", "gy", "gz"),
            P(None, "gx", "gy", "gz"),
            P("gx", "gy", "gz"),
            P("gz", "gx", "gy", None),
            P(),
            P("gz"),
            P("gz", None, None, None, None),
        ),
        out_specs=(
            P(None, "gx", "gy", "gz"),
            P(None, "gx", "gy", "gz"),
            P("gz", "gx", "gy", None),
            P(("gx", "gy"), "gz", None),
        ),
        check_vma=False,
    )
```

```python
import jax
import jax.numpy as jnp
from jax import lax
from jax.sharding import PartitionSpec as P
from jax.experimental.layout import Layout, with_layout_constraint

STEPS = 2
NF = 16
MODES = 2
HALO = 2
AXES = ("gx", "gy", "gz")


def pin(value):
    return with_layout_constraint(value, Layout(tuple(range(value.ndim))))


def shifted(value, axis, steps):
    count = lax.axis_size(axis)
    first, last = (max(0, -steps), min(count, count - steps))
    return lax.ppermute(value, axis, [(source, source + steps) for source in range(first, last)])


def widen(stack, dim, axis):
    count = stack.shape[dim]
    low = lax.slice_in_dim(stack, 0, HALO, axis=dim)
    high = lax.slice_in_dim(stack, count - HALO, count, axis=dim)
    from_below = shifted(high, axis, 1)
    from_above = shifted(low, axis, -1)
    return jnp.concatenate([from_below, stack, from_above], axis=dim)


def widen_lanes(stack, axis):
    lanes = stack.shape[-1]
    flat = stack.reshape(-1, lanes)
    lane = jnp.arange(lanes)
    edges = jnp.concatenate([jnp.arange(HALO), jnp.arange(lanes - HALO, lanes)])
    pick = (lane[None, :] == edges[:, None]).astype(jnp.float32)
    faces = jnp.einsum("kz,rz->kr", pick, flat, precision=lax.Precision.HIGH)
    from_above = shifted(faces[:HALO], axis, -1)
    from_below = shifted(faces[HALO:], axis, 1)
    ghosts = jnp.concatenate([from_below, from_above], axis=0)
    out = jnp.arange(lanes + 2 * HALO)
    spots = jnp.concatenate([jnp.arange(HALO), jnp.arange(lanes + HALO, lanes + 2 * HALO)])
    move = (out[None, :] == lane[:, None] + HALO).astype(jnp.float32)
    place = (out[None, :] == spots[:, None]).astype(jnp.float32)
    wide = jnp.dot(flat, move, precision=lax.Precision.HIGH) + jnp.einsum(
        "kr,kl->rl", ghosts, place, precision=lax.Precision.HIGH
    )
    return wide.reshape(stack.shape[:-1] + (lanes + 2 * HALO,))


def box(value, start, size):
    lead = value.ndim - 3
    return lax.slice(
        value,
        (0,) * lead + tuple(start),
        value.shape[:lead] + tuple(s + n for s, n in zip(start, size)),
    )


def moved(start, dim, step):
    return tuple(s + step if d == dim else s for d, s in enumerate(start))


def differ(value, start, size, dim, step):
    if step > 0:
        return box(value, moved(start, dim, 1), size) - box(value, start, size)
    return box(value, start, size) - box(value, moved(start, dim, -1), size)


def curl(field, start, size, step):
    vx, vy, vz = field
    d = lambda v, dim: differ(v, start, size, dim, step)
    return [d(vz, 1) - d(vy, 2), d(vx, 2) - d(vz, 0), d(vy, 0) - d(vx, 1)]


def inside(origin, size, cells):
    masks = []
    for dim, axis in enumerate(AXES):
        count = lax.axis_size(axis)
        first = lax.axis_index(axis) * cells[dim] + origin
        where = first + jnp.arange(size[dim])
        masks.append((where >= 0) & (where < count * cells[dim]))
    return (
        masks[0][:, None, None] & masks[1][None, :, None] & masks[2][None, None, :]
    ).astype(jnp.float32)


def per_device(e_field, h_field, inv_permittivity, dft_sums, omega, port_z, mode_profiles):
    cells = e_field.shape[1:]
    cells_x, cells_y, cells_z = cells
    ports_here = dft_sums.shape[0]
    stack = jnp.concatenate([e_field, h_field, inv_permittivity[None]], axis=0)
    stack = pin(widen(stack, 2, "gy"))
    stack = widen(stack, 1, "gx")
    spare = -stack.shape[2] % 8
    stack = pin(jnp.pad(stack, ((0, 0), (0, 0), (0, spare), (0, 0))))
    stack = pin(widen_lanes(stack, "gz"))
    e0 = [stack[i] for i in range(3)]
    h0 = [stack[3 + i] for i in range(3)]
    inv = stack[6]
    n = lambda k: tuple(c + k for c in cells)
    at = lambda v, k, size: box(v, (k, k, k), size)
    keep = inside(-2, n(3), cells)
    h1 = [pin((at(v, 0, n(3)) - 0.5 * c) * keep) for v, c in zip(h0, curl(e0, (0, 0, 0), n(3), 1))]
    scale = 0.5 * at(inv, 1, n(2))
    e1 = [pin(at(v, 1, n(2)) + scale * c) for v, c in zip(e0, curl(h1, (1, 1, 1), n(2), -1))]
    keep = inside(-1, n(1), cells)
    h2 = [pin((at(v, 1, n(1)) - 0.5 * c) * keep) for v, c in zip(h1, curl(e1, (0, 0, 0), n(1), 1))]
    scale = 0.5 * at(inv, 2, n(0))
    e2 = [at(v, 1, n(0)) + scale * c for v, c in zip(e1, curl(h2, (1, 1, 1), n(0), -1))]
    e1_here = [at(v, 1, n(0)) for v in e1]
    h1_here = [at(v, 2, n(0)) for v in h1]
    h2_here = [at(v, 1, n(0)) for v in h2]
    local_z = port_z - lax.axis_index("gz") * cells_z
    onehot = (local_z[:, None] == jnp.arange(cells_z)[None, :]).astype(jnp.float32)
    lanes = dft_sums.shape[-1]
    lane_part = jnp.arange(lanes) // (lanes // 4)
    spread_of = (lane_part[None, :] == jnp.arange(4)[:, None]).astype(jnp.float32)
    dft = dft_sums
    for step, (e_now, h_now) in enumerate(((e1_here, h1_here), (e2, h2_here))):
        tangent = pin(jnp.stack([e_now[0], e_now[1], h_now[0], h_now[1]]))
        planes = jnp.sum(tangent[None] * onehot[:, None, None, None, :], axis=-1)
        phase = omega * jnp.float32(step + 1)
        trig = jnp.stack([jnp.cos(phase), jnp.sin(phase)])
        coef = jnp.tile(trig.reshape(-1), 4)
        spread = jnp.sum(planes[..., None] * spread_of[None, :, None, None, :], axis=1)
        dft = pin(dft + spread * coef)
    groups = lax.axis_size(("gx", "gy"))
    owned = ports_here * NF // groups
    start_x = lax.axis_index("gx") * cells_x
    start_y = lax.axis_index("gy") * cells_y
    tile = lax.dynamic_slice(
        mode_profiles, (0, 0, 0, start_x, start_y), (ports_here, MODES, 4, cells_x, cells_y)
    )
    weights = tile.reshape(ports_here, MODES * 4, cells_x, cells_y).astype(jnp.float32)
    crossed = jnp.einsum("pxyl,pnxy->pnl", dft, weights, precision=lax.Precision.HIGHEST)
    crossed = crossed.reshape(ports_here, MODES, 4, 4, 2, NF)
    diagonal = sum(crossed[:, :, c, c] for c in range(4))
    partial_sums = jnp.transpose(diagonal, (0, 3, 1, 2)).reshape(ports_here * NF, MODES * 2)
    pieces = partial_sums.reshape(groups, owned, MODES * 2)
    result = jnp.sum(lax.all_to_all(pieces, ("gx", "gy"), 0, 0, tiled=False), axis=0)
    return (jnp.stack(e2), jnp.stack(h2_here), dft, result.reshape(owned, 1, MODES * 2))


def solution(mesh):
    return jax.shard_map(
        per_device,
        mesh=mesh,
        in_specs=(
            P(None, "gx", "gy", "gz"),
            P(None, "gx", "gy", "gz"),
            P("gx", "gy", "gz"),
            P("gz", "gx", "gy", None),
            P(),
            P("gz"),
            P("gz", None, None, None, None),
        ),
        out_specs=(
            P(None, "gx", "gy", "gz"),
            P(None, "gx", "gy", "gz"),
            P("gz", "gx", "gy", None),
            P(("gx", "gy"), "gz", None),
        ),
        check_vma=False,
    )
```
